128 devices in a mesh: batch: 16 (over y, x), table: 8 (over z, core).
Axes of the slice: x: 4, y: 4, z: 4, core: 2. Of those that a mesh axis runs over, the one named last changes fastest.
Arguments:
- item_table: bfloat16 [262144, 256], P(('batch', 'table'))
- query_table: bfloat16 [8192, 256], replicated, may hold values from -15 to 15
- query_weight: bfloat16 [256, 256], replicated, may hold values from -0.375 to 0.375
- query_ids: int32 [65536, 8], P(('batch', 'table')), may hold values from 0 to 8191
- fetch_rows: int32 [128, 128, 8], P(('batch', 'table')), may hold values from 0 to 2047, as said below
- counts: int32 [128, 128], P(('batch', 'table')), may hold values from 1 to 8, as said below
- example_pos: int32 [65536], P(('batch', 'table')), may hold values from 0 to 1023, as said below
Outputs:
- table_grad: float32 [262144, 256], P(('batch', 'table'))
- weight_grad: float32 [256, 256], replicated
The draws below stay inside these ranges and needn't reach their ends.
Inputs may be any that keep to these rules, and one draw needn't show every extreme that they name: `fetch_rows`: for each device and owner, the 8 listed rows are distinct; only the first counts of them are live. `counts`: one owner, drawn from the seed, receives 8 live slots from every device; one device, drawn from the seed, has 8 live slots to every owner. `example_pos`: each example's position is below the sum of its device's counts; positions repeat.
All inputs are finite; a program needn't handle non-finite values.
Results may differ from the reference program's by a relative error of at most 0.005.
Values may be sent and summed in bfloat16 or wider, within the bound.
No kernel may reach another device: no remote copies, remote signals or barrier semaphores. Data moves between devices by JAX's collectives and lax.ppermute only.
A program may use at most 128 MiB of HBM per device.

```python
import math
import jax
import jax.numpy as jnp
import numpy as np
from jax import lax

D = 256
QV = 8192
F = 8
B_DEV = 512
ROWS_DEV = 2048
SOURCES = 128
CAP = 8
EXAMPLES = 65536
ROWS = 262144
GROUP = 8192
N_BATCH = 16
N_TABLE = 8


def draw_live(key):
    hottest = jax.random.randint(jax.random.fold_in(key, 11), (), 0, SOURCES)
    fullest = jax.random.randint(jax.random.fold_in(key, 13), (), 0, SOURCES)
    drawn = jax.random.randint(jax.random.fold_in(key, 12), (SOURCES, SOURCES), 1, CAP + 1)
    owners = jnp.arange(SOURCES, dtype=jnp.int32)
    filled = (owners[None, :] == hottest) | (owners[:, None] == fullest)
    return jnp.where(filled, CAP, drawn).astype(jnp.int32)


def draw_counts(key, part):
    return draw_live(key)


def draw_example_pos(key, part):
    live = draw_live(key)
    overall = jnp.sum(live, axis=1, keepdims=True).astype(jnp.int32)
    spread_pos = jax.random.randint(jax.random.fold_in(key, 21), (SOURCES, B_DEV), 0, overall)
    narrow_pos = jax.random.randint(jax.random.fold_in(key, 22), (SOURCES, B_DEV), 0, jnp.maximum(overall // 16, 1))
    picker = jax.random.randint(jax.random.fold_in(key, 23), (SOURCES, B_DEV), 0, 4)
    chosen = jnp.where(picker == 0, narrow_pos, spread_pos).astype(jnp.int32)
    columns = jnp.arange(B_DEV, dtype=jnp.int32)[None, :]
    chosen = jnp.where(columns == B_DEV - 1, overall - 1, chosen)
    return chosen.astype(jnp.int32).reshape(-1)


def draw_fetch_rows(key, part):
    opening = jax.random.randint(jax.random.fold_in(key, 31), (SOURCES, SOURCES, 1), 0, ROWS_DEV)
    picker = jax.random.randint(jax.random.fold_in(key, 32), (SOURCES, SOURCES, 1), 0, 4)
    primes = jnp.array([1000003, 999983, 1000033, 999979], jnp.int32)
    strides = jnp.take(primes, picker) % ROWS_DEV
    counter = jnp.arange(CAP, dtype=jnp.int32)[None, None, :]
    return ((opening + counter * strides) % ROWS_DEV).astype(jnp.int32)


def draw_item_table(key, part):
    values = jnp.clip(jax.random.normal(jax.random.fold_in(key, 44), (ROWS, D), jnp.float32), -6.0, 6.0)
    return values.astype(jnp.bfloat16)


def plant(values, rng, least, high):
    spot = [jax.random.randint(jax.random.fold_in(rng, axis), (), 0, length) for axis, length in enumerate(values.shape)]
    widest = values.shape.index(max(values.shape))
    neighbour = spot[:widest] + [(spot[widest] + 1) % values.shape[widest]] + spot[widest + 1:]
    return values.at[tuple(spot)].set(least).at[tuple(neighbour)].set(high)


def rank_table(count, skew):
    weights = [(1 << 20) // math.isqrt(standing ** skew) + 1 for standing in range(1, count + 1)]
    deviation = 1 + sum(weights) // (1 << 30)
    return np.cumsum(np.array([max(1, weight // deviation) for weight in weights]))


def ranked(stream_key, dims, count, slope):
    listing = rank_table(count, slope)
    ticket = jax.random.randint(jax.random.fold_in(stream_key, 1), dims, 0, int(listing[count - 1]))
    standing = jnp.searchsorted(jnp.asarray(listing, jnp.int32), ticket, side="right")
    return jax.random.permutation(jax.random.fold_in(stream_key, 2), count)[standing].astype(jnp.int32)


def scatter_about(own_key, shape, width, limit, kind=jnp.bfloat16):
    return jnp.clip(width * jax.random.normal(own_key, shape, jnp.float32), -limit, limit).astype(kind)


def setup_inputs(seed: int = 0) -> dict:
    arg_keys = jax.random.split(jax.random.key(seed), 8)
    item_table = draw_item_table(jax.random.fold_in(arg_keys[7], 71), 0)
    query_table = scatter_about(arg_keys[1], (QV, D), 2.5, 15.0)
    query_weight = scatter_about(arg_keys[2], (D, D), D ** -0.5, 0.375)
    query_ids = plant(ranked(arg_keys[3], (EXAMPLES, F), QV, 2), jax.random.fold_in(arg_keys[3], 3), 0, QV - 1).astype(jnp.int32)
    fetch_rows = draw_fetch_rows(jax.random.fold_in(arg_keys[7], 71), 0)
    counts = draw_counts(jax.random.fold_in(arg_keys[7], 71), 0)
    example_pos = draw_example_pos(jax.random.fold_in(arg_keys[7], 71), 0)
    return dict(item_table=item_table, query_table=query_table, query_weight=query_weight, query_ids=query_ids, fetch_rows=fetch_rows, counts=counts, example_pos=example_pos)


def slot_index(live_slots, positions):
    ending = jnp.cumsum(live_slots).astype(jnp.int32)
    holder = jnp.sum((ending[None, :] <= positions[:, None]).astype(jnp.int32), axis=1).astype(jnp.int32)
    opening = (ending - live_slots).astype(jnp.int32)
    return (holder * CAP + positions - jnp.take(opening, holder)).astype(jnp.int32)


def reference(item_table, query_table, query_weight, query_ids, fetch_rows, counts, example_pos):
    scaling = D ** -0.5
    owners = jnp.arange(SOURCES, dtype=jnp.int32)
    rows_global = (owners[None, :, None] * ROWS_DEV + fetch_rows).astype(jnp.int32)
    fetched = jnp.take(item_table, rows_global.reshape(-1), axis=0).reshape(SOURCES, SOURCES * CAP, D)
    positions = example_pos.reshape(SOURCES, B_DEV)
    slot_ids = jax.vmap(slot_index)(counts, positions)
    item_vectors = jax.vmap(lambda rows_here, wanted: jnp.take(rows_here, wanted, axis=0))(fetched, slot_ids)

    def tower(ids_here):
        looked = jnp.take(query_table, ids_here, axis=0).astype(jnp.float32)
        return jnp.mean(looked, axis=1).astype(jnp.bfloat16)

    hidden = lax.map(tower, query_ids.reshape(SOURCES, B_DEV, F))
    queries = jnp.dot(hidden.reshape(-1, D), query_weight, preferred_element_type=jnp.float32)
    queries = queries.astype(jnp.bfloat16).reshape(SOURCES, B_DEV, D)

    def to_groups(array):
        return array.reshape(N_BATCH, N_TABLE, B_DEV, D).transpose(1, 0, 2, 3).reshape(N_TABLE, GROUP, D)

    def from_groups(array):
        return array.reshape(N_TABLE, N_BATCH, B_DEV, D).transpose(1, 0, 2, 3).reshape(SOURCES, B_DEV, D)

    group_queries = to_groups(queries)
    group_items = to_groups(item_vectors)

    def group_grads(pair):
        query_group, item_group = pair

        def one_block(accum, query_rows):
            scores = scaling * jnp.dot(query_rows, item_group.T, preferred_element_type=jnp.float32)
            highest = jnp.max(scores, axis=1, keepdims=True)
            totals = highest + jnp.log(jnp.sum(jnp.exp(scores - highest), axis=1, keepdims=True))
            soft_weights = jnp.exp(scores - totals).astype(jnp.bfloat16)
            pulled = jnp.dot(soft_weights, item_group, preferred_element_type=jnp.float32)
            accum = accum + jnp.dot(soft_weights.T, query_rows, preferred_element_type=jnp.float32)
            return accum, pulled

        accum, pulled = lax.scan(one_block, jnp.zeros((GROUP, D), jnp.float32), query_group.reshape(N_BATCH, B_DEV, D))
        return accum, pulled.reshape(GROUP, D)

    accum, pulled = lax.map(group_grads, (group_queries, group_items))
    query_grad = from_groups(scaling * (pulled - group_items.astype(jnp.float32)))
    item_grad = from_groups(scaling * (accum - group_queries.astype(jnp.float32)))
    slot_grads = jax.vmap(lambda grads_here, wanted: jax.ops.segment_sum(grads_here, wanted, num_segments=SOURCES * CAP))(item_grad, slot_ids)
    table_grad = jnp.zeros((ROWS, D), jnp.float32).at[rows_global.reshape(-1)].add(slot_grads.reshape(-1, D))
    query_grad_low = query_grad.astype(jnp.bfloat16).reshape(-1, D)
    weight_grad = jnp.dot(hidden.reshape(-1, D).T, query_grad_low, preferred_element_type=jnp.float32)
    return table_grad, weight_grad
```

```python
import jax
import jax.numpy as jnp
from jax import lax
from jax.sharding import PartitionSpec as P


def slot_index(live_slots, positions, slot_cap):
    ending = jnp.cumsum(live_slots)
    holder = jnp.sum((ending[None, :] <= positions[:, None]).astype(jnp.int32), axis=1)
    opening = ending - live_slots
    return holder * slot_cap + positions - jnp.take(opening, holder)


def butterfly_sum(value, axes):
    total = 1
    for axis in axes:
        total *= lax.axis_size(axis)
    step = 1
    while step < total:
        pairs = [(i, i ^ step) for i in range(total)]
        value = value + lax.ppermute(value, axes, pairs)
        step *= 2
    return value


def local(item_table, query_table, query_weight, query_ids, fetch_rows, counts, example_pos):
    table_rows, model_width = item_table.shape
    sources = fetch_rows.shape[1]
    slot_cap = fetch_rows.shape[2]
    scaling = model_width ** (-0.5)
    requests = fetch_rows.reshape(sources, slot_cap)
    wanted = lax.all_to_all(requests, ("batch", "table"), split_axis=0, concat_axis=0, tiled=True)
    found_rows = jnp.take(item_table, wanted, axis=0)
    fetched = lax.all_to_all(
        found_rows, ("batch", "table"), split_axis=0, concat_axis=0, tiled=True
    )
    slot_ids = slot_index(counts.reshape(sources), example_pos, slot_cap)
    item_vectors = jnp.take(fetched.reshape(sources * slot_cap, model_width), slot_ids, axis=0)
    looked = jnp.take(query_table, query_ids, axis=0).astype(jnp.float32)
    hidden = jnp.mean(looked, axis=1).astype(jnp.bfloat16)
    queries = jnp.dot(hidden, query_weight, preferred_element_type=jnp.float32).astype(jnp.bfloat16)
    group_items = lax.all_gather(item_vectors, "batch", axis=0, tiled=True)
    scores = scaling * lax.dot_general(
        queries, group_items, (((1,), (1,)), ((), ())), preferred_element_type=jnp.float32
    )
    highest = jnp.max(scores, axis=1, keepdims=True)
    totals = highest + jnp.log(jnp.sum(jnp.exp(scores - highest), axis=1, keepdims=True))
    soft_weights = jnp.exp(scores - totals).astype(jnp.bfloat16)
    pulled = jnp.dot(soft_weights, group_items, preferred_element_type=jnp.float32)
    query_grad = scaling * (pulled - item_vectors.astype(jnp.float32))
    term_rows = lax.dot_general(
        soft_weights, queries, (((0,), (0,)), ((), ())), preferred_element_type=jnp.float32
    )
    summed = lax.psum_scatter(term_rows, "batch", scatter_dimension=0, tiled=True)
    item_grad = scaling * (summed - queries.astype(jnp.float32))
    slot_grads = jax.ops.segment_sum(item_grad, slot_ids, num_segments=sources * slot_cap)
    slot_grads = slot_grads.reshape(sources, slot_cap, model_width)
    returned = lax.all_to_all(
        slot_grads, ("batch", "table"), split_axis=0, concat_axis=0, tiled=True
    )
    table_grad = (
        jnp.zeros((table_rows, model_width), jnp.float32)
        .at[wanted.reshape(-1)]
        .add(returned.reshape(-1, model_width))
    )
    partial_value = lax.dot_general(
        hidden,
        query_grad.astype(jnp.bfloat16),
        (((0,), (0,)), ((), ())),
        preferred_element_type=jnp.float32,
    )
    weight_grad = butterfly_sum(partial_value, ("batch", "table"))
    return (table_grad, weight_grad)


def solution(mesh):
    in_specs = (
        P(("batch", "table"), None),
        P(),
        P(),
        P(("batch", "table"), None),
        P(("batch", "table"), None, None),
        P(("batch", "table"), None),
        P(("batch", "table")),
    )
    out_specs = (P(("batch", "table"), None), P())
    return jax.shard_map(local, mesh=mesh, in_specs=in_specs, out_specs=out_specs, check_vma=False)
```

```python
import jax
import jax.numpy as jnp
from jax import lax
from jax.sharding import PartitionSpec as P


def slot_index(live_slots, positions, slot_cap):
    ending = jnp.cumsum(live_slots)
    holder = jnp.sum((ending[None, :] <= positions[:, None]).astype(jnp.int32), axis=1)
    opening = ending - live_slots
    return holder * slot_cap + positions - jnp.take(opening, holder)


def butterfly_sum(value, axes):
    total = 1
    for axis in axes:
        total *= lax.axis_size(axis)
    step = 1
    while step < total:
        pairs = [(i, i ^ step) for i in range(total)]
        value = value + lax.ppermute(value, axes, pairs)
        step *= 2
    return value


def local(item_table, query_table, query_weight, query_ids, fetch_rows, counts, example_pos):
    table_rows, model_width = item_table.shape
    sources = fetch_rows.shape[1]
    slot_cap = fetch_rows.shape[2]
    scaling = model_width ** (-0.5)
    requests = fetch_rows.reshape(sources, slot_cap)
    wanted = lax.all_to_all(requests, ("batch", "table"), split_axis=0, concat_axis=0, tiled=True)
    found_rows = jnp.take(item_table, wanted, axis=0)
    fetched = lax.all_to_all(
        found_rows, ("batch", "table"), split_axis=0, concat_axis=0, tiled=True
    )
    slot_ids = slot_index(counts.reshape(sources), example_pos, slot_cap)
    item_vectors = jnp.take(fetched.reshape(sources * slot_cap, model_width), slot_ids, axis=0)
    looked = jnp.take(query_table, query_ids, axis=0).astype(jnp.float32)
    hidden = jnp.mean(looked, axis=1).astype(jnp.bfloat16)
    queries = jnp.dot(hidden, query_weight, preferred_element_type=jnp.float32).astype(jnp.bfloat16)
    group_queries = lax.all_gather(queries, "batch", axis=0, tiled=True)
    group_items = lax.all_gather(item_vectors, "batch", axis=0, tiled=True)
    scores = scaling * lax.dot_general(
        queries, group_items, (((1,), (1,)), ((), ())), preferred_element_type=jnp.float32
    )
    highest = jnp.max(scores, axis=1, keepdims=True)
    totals = highest + jnp.log(jnp.sum(jnp.exp(scores - highest), axis=1, keepdims=True))
    soft_weights = jnp.exp(scores - totals).astype(jnp.bfloat16)
    pulled = jnp.dot(soft_weights, group_items, preferred_element_type=jnp.float32)
    query_grad = scaling * (pulled - item_vectors.astype(jnp.float32))
    group_totals = lax.all_gather(totals.reshape(1, -1), "batch", axis=1, tiled=True)
    scores_back = scaling * lax.dot_general(
        item_vectors, group_queries, (((1,), (1,)), ((), ())), preferred_element_type=jnp.float32
    )
    soft_back = jnp.exp(scores_back - group_totals).astype(jnp.bfloat16)
    summed = jnp.dot(soft_back, group_queries, preferred_element_type=jnp.float32)
    item_grad = scaling * (summed - queries.astype(jnp.float32))
    slot_grads = jax.ops.segment_sum(item_grad, slot_ids, num_segments=sources * slot_cap)
    slot_grads = slot_grads.reshape(sources, slot_cap, model_width)
    returned = lax.all_to_all(
        slot_grads, ("batch", "table"), split_axis=0, concat_axis=0, tiled=True
    )
    table_grad = (
        jnp.zeros((table_rows, model_width), jnp.float32)
        .at[wanted.reshape(-1)]
        .add(returned.reshape(-1, model_width))
    )
    partial_value = lax.dot_general(
        hidden,
        query_grad.astype(jnp.bfloat16),
        (((0,), (0,)), ((), ())),
        preferred_element_type=jnp.float32,
    )
    weight_grad = butterfly_sum(partial_value, ("batch", "table"))
    return (table_grad, weight_grad)


def solution(mesh):
    in_specs = (
        P(("batch", "table"), None),
        P(),
        P(),
        P(("batch", "table"), None),
        P(("batch", "table"), None, None),
        P(("batch", "table"), None),
        P(("batch", "table")),
    )
    out_specs = (P(("batch", "table"), None), P())
    return jax.shard_map(local, mesh=mesh, in_specs=in_specs, out_specs=out_specs, check_vma=False)
```

```python
import functools

import jax
import jax.numpy as jnp
from jax import lax
from jax.experimental import pallas as pl
from jax.experimental.pallas import tpu as pltpu
from jax.sharding import PartitionSpec as P


def forward_block(q_ref, items_ref, own_ref, grad_ref, totals_ref, *, scaling):
    scores = scaling * lax.dot_general(
        q_ref[...], items_ref[...], (((1,), (1,)), ((), ())), preferred_element_type=jnp.float32
    )
    highest = jnp.max(scores, axis=1, keepdims=True)
    totals = highest + jnp.log(jnp.sum(jnp.exp(scores - highest), axis=1, keepdims=True))
    soft_weights = jnp.exp(scores - totals).astype(jnp.bfloat16)
    pulled = jnp.dot(soft_weights, items_ref[...], preferred_element_type=jnp.float32)
    grad_ref[...] = scaling * (pulled - own_ref[...].astype(jnp.float32))
    totals_ref[...] = jnp.broadcast_to(totals, totals_ref.shape)


def forward(queries, group_items, item_vectors, tile=256):
    rows, width = queries.shape
    group = group_items.shape[0]
    return pl.pallas_call(
        functools.partial(forward_block, scaling=width ** (-0.5)),
        grid=(rows // tile,),
        in_specs=[
            pl.BlockSpec((tile, width), lambda i: (i, 0)),
            pl.BlockSpec((group, width), lambda i: (0, 0)),
            pl.BlockSpec((tile, width), lambda i: (i, 0)),
        ],
        out_specs=[
            pl.BlockSpec((tile, width), lambda i: (i, 0)),
            pl.BlockSpec((tile, 128), lambda i: (i, 0)),
        ],
        out_shape=[
            jax.ShapeDtypeStruct((rows, width), jnp.float32),
            jax.ShapeDtypeStruct((rows, 128), jnp.float32),
        ],
        compiler_params=pltpu.CompilerParams(vmem_limit_bytes=48 * 1024 * 1024),
    )(queries, group_items, item_vectors)


def plane_gather(value, axis, side):
    size = side * side
    index = lax.axis_index(axis)
    column = index % side
    line = index // side

    def shift(piece, step, along_row):
        pairs = []
        for source in range(size):
            high, low = divmod(source, side)
            if along_row:
                target = high * side + (low + step) % side
            else:
                target = ((high + step) % side) * side + low
            pairs.append((source, target))
        return lax.ppermute(piece, axis, pairs)

    pieces = jnp.stack([value] + [shift(value, step, True) for step in range(1, side)])
    row = jnp.concatenate([jnp.take(pieces, (column - c) % side, axis=0) for c in range(side)], axis=1)
    rows = jnp.stack([row] + [shift(row, step, False) for step in range(1, side)])
    return jnp.concatenate([jnp.take(rows, (line - r) % side, axis=0) for r in range(side)], axis=1)


def slot_index(live_slots, positions, slot_cap):
    ending = jnp.cumsum(live_slots)
    holder = jnp.sum((ending[None, :] <= positions[:, None]).astype(jnp.int32), axis=1)
    opening = ending - live_slots
    return holder * slot_cap + positions - jnp.take(opening, holder)


def butterfly_sum(value, axes):
    total = 1
    for axis in axes:
        total *= lax.axis_size(axis)
    step = 1
    while step < total:
        pairs = [(i, i ^ step) for i in range(total)]
        value = value + lax.ppermute(value, axes, pairs)
        step *= 2
    return value


def local(item_table, query_table, query_weight, query_ids, fetch_rows, counts, example_pos):
    table_rows, model_width = item_table.shape
    sources = fetch_rows.shape[1]
    slot_cap = fetch_rows.shape[2]
    scaling = model_width ** (-0.5)
    requests = fetch_rows.reshape(sources, slot_cap)
    wanted = lax.all_to_all(requests, ("batch", "table"), split_axis=0, concat_axis=0, tiled=True)
    found_rows = jnp.take(item_table, wanted, axis=0)
    fetched = lax.all_to_all(
        found_rows, ("batch", "table"), split_axis=0, concat_axis=0, tiled=True
    )
    slot_ids = slot_index(counts.reshape(sources), example_pos, slot_cap)
    item_vectors = jnp.take(fetched.reshape(sources * slot_cap, model_width), slot_ids, axis=0)
    looked = jnp.take(query_table, query_ids, axis=0).astype(jnp.float32)
    hidden = jnp.mean(looked, axis=1).astype(jnp.bfloat16)
    queries = jnp.dot(hidden, query_weight, preferred_element_type=jnp.float32).astype(jnp.bfloat16)
    group_queries = lax.all_gather(queries, "batch", axis=0, tiled=True)
    group_items = lax.all_gather(item_vectors, "batch", axis=0, tiled=True)
    query_grad, totals = forward(queries, group_items, item_vectors)
    side = int(round(lax.axis_size("batch") ** 0.5))
    if side * side == lax.axis_size("batch"):
        group_totals = plane_gather(totals[:, :1].reshape(1, -1), "batch", side)
    else:
        group_totals = lax.all_gather(totals[:, :1].reshape(1, -1), "batch", axis=1, tiled=True)
    scores_back = scaling * lax.dot_general(
        item_vectors, group_queries, (((1,), (1,)), ((), ())), preferred_element_type=jnp.float32
    )
    soft_back = jnp.exp(scores_back - group_totals).astype(jnp.bfloat16)
    summed = jnp.dot(soft_back, group_queries, preferred_element_type=jnp.float32)
    item_grad = scaling * (summed - queries.astype(jnp.float32))
    slot_grads = jax.ops.segment_sum(item_grad, slot_ids, num_segments=sources * slot_cap)
    slot_grads = slot_grads.reshape(sources, slot_cap, model_width)
    returned = lax.all_to_all(
        slot_grads, ("batch", "table"), split_axis=0, concat_axis=0, tiled=True
    )
    table_grad = (
        jnp.zeros((table_rows, model_width), jnp.float32)
        .at[wanted.reshape(-1)]
        .add(returned.reshape(-1, model_width))
    )
    partial_value = lax.dot_general(
        hidden,
        query_grad.astype(jnp.bfloat16),
        (((0,), (0,)), ((), ())),
        preferred_element_type=jnp.float32,
    )
    weight_grad = butterfly_sum(partial_value, ("batch", "table"))
    return (table_grad, weight_grad)


def solution(mesh):
    in_specs = (
        P(("batch", "table"), None),
        P(),
        P(),
        P(("batch", "table"), None),
        P(("batch", "table"), None, None),
        P(("batch", "table"), None),
        P(("batch", "table")),
    )
    out_specs = (P(("batch", "table"), None), P())
    return jax.shard_map(local, mesh=mesh, in_specs=in_specs, out_specs=out_specs, check_vma=False)
```

```python
import functools

import jax
import jax.numpy as jnp
from jax import lax
from jax.experimental import pallas as pl
from jax.experimental.pallas import tpu as pltpu
from jax.sharding import PartitionSpec as P


def forward_block(q_ref, items_ref, own_ref, grad_ref, totals_ref, *, scaling):
    scores = scaling * lax.dot_general(
        q_ref[...], items_ref[...], (((1,), (1,)), ((), ())), preferred_element_type=jnp.float32
    )
    highest = jnp.max(scores, axis=1, keepdims=True)
    totals = highest + jnp.log(jnp.sum(jnp.exp(scores - highest), axis=1, keepdims=True))
    soft_weights = jnp.exp(scores - totals).astype(jnp.bfloat16)
    pulled = jnp.dot(soft_weights, items_ref[...], preferred_element_type=jnp.float32)
    grad_ref[...] = scaling * (pulled - own_ref[...].astype(jnp.float32))
    totals_ref[...] = jnp.broadcast_to(totals, totals_ref.shape)


def forward(queries, group_items, item_vectors, tile=256):
    rows, width = queries.shape
    group = group_items.shape[0]
    return pl.pallas_call(
        functools.partial(forward_block, scaling=width ** (-0.5)),
        grid=(rows // tile,),
        in_specs=[
            pl.BlockSpec((tile, width), lambda i: (i, 0)),
            pl.BlockSpec((group, width), lambda i: (0, 0)),
            pl.BlockSpec((tile, width), lambda i: (i, 0)),
        ],
        out_specs=[
            pl.BlockSpec((tile, width), lambda i: (i, 0)),
            pl.BlockSpec((tile, 128), lambda i: (i, 0)),
        ],
        out_shape=[
            jax.ShapeDtypeStruct((rows, width), jnp.float32),
            jax.ShapeDtypeStruct((rows, 128), jnp.float32),
        ],
        compiler_params=pltpu.CompilerParams(vmem_limit_bytes=48 * 1024 * 1024),
    )(queries, group_items, item_vectors)


def plane_gather(value, axis, side):
    size = side * side
    index = lax.axis_index(axis)
    column = index % side
    line = index // side

    def shift(piece, step, along_row):
        pairs = []
        for source in range(size):
            high, low = divmod(source, side)
            if along_row:
                target = high * side + (low + step) % side
            else:
                target = ((high + step) % side) * side + low
            pairs.append((source, target))
        return lax.ppermute(piece, axis, pairs)

    pieces = jnp.stack([value] + [shift(value, step, True) for step in range(1, side)])
    row = jnp.concatenate([jnp.take(pieces, (column - c) % side, axis=0) for c in range(side)], axis=1)
    rows = jnp.stack([row] + [shift(row, step, False) for step in range(1, side)])
    return jnp.concatenate([jnp.take(rows, (line - r) % side, axis=0) for r in range(side)], axis=1)


def slot_index(live_slots, positions, slot_cap):
    ending = jnp.cumsum(live_slots)
    holder = jnp.sum((ending[None, :] <= positions[:, None]).astype(jnp.int32), axis=1)
    opening = ending - live_slots
    return holder * slot_cap + positions - jnp.take(opening, holder)


def butterfly_sum(value, axes):
    total = 1
    for axis in axes:
        total *= lax.axis_size(axis)
    step = 1
    while step < total:
        pairs = [(i, i ^ step) for i in range(total)]
        value = value + lax.ppermute(value, axes, pairs)
        step *= 2
    return value


def plane_shift(value, axis, side, step, along_row):
    pairs = []
    for source in range(side * side):
        high, low = divmod(source, side)
        if along_row:
            target = high * side + (low + step) % side
        else:
            target = ((high + step) % side) * side + low
        pairs.append((source, target))
    return lax.ppermute(value, axis, pairs)


def plane_gather_rows(value, axis, side, along_row):
    pieces = [value] + [plane_shift(value, axis, side, step, along_row) for step in range(1, side)]
    return jnp.concatenate(pieces, axis=0)


def plane_reduce_rows(value, axis, side, along_row):
    block = value.shape[0] // side
    total = value[:block]
    for step in range(1, side):
        part = value[((side - step) % side) * block:((side - step) % side + 1) * block]
        total = total + plane_shift(part, axis, side, step, along_row)
    return total


def block_grads(queries, item_vectors, axis, side, scaling):
    row_queries = plane_gather_rows(queries, axis, side, True)
    column_items = plane_gather_rows(item_vectors, axis, side, False)
    scores = scaling * lax.dot_general(
        row_queries, column_items, (((1,), (1,)), ((), ())), preferred_element_type=jnp.float32
    )
    local_max = jnp.max(scores, axis=1)
    local_sum = jnp.sum(jnp.exp(scores - local_max[:, None]), axis=1)
    stats = jnp.stack([local_max, local_sum])
    block = queries.shape[0]
    gathered = [stats] + [
        jnp.roll(plane_shift(stats, axis, side, step, True), step * block, axis=1) for step in range(1, side)
    ]
    highest = gathered[0][0]
    for other in gathered[1:]:
        highest = jnp.maximum(highest, other[0])
    mass = gathered[0][1] * jnp.exp(gathered[0][0] - highest)
    for other in gathered[1:]:
        mass = mass + other[1] * jnp.exp(other[0] - highest)
    totals = highest + jnp.log(mass)
    soft_weights = jnp.exp(scores - totals[:, None]).astype(jnp.bfloat16)
    pulled = jnp.dot(soft_weights, column_items, preferred_element_type=jnp.float32)
    pushed = lax.dot_general(
        soft_weights, row_queries, (((0,), (0,)), ((), ())), preferred_element_type=jnp.float32
    )
    pulled = plane_reduce_rows(pulled, axis, side, True)
    pushed = plane_reduce_rows(pushed, axis, side, False)
    query_grad = scaling * (pulled - item_vectors.astype(jnp.float32))
    item_grad = scaling * (pushed - queries.astype(jnp.float32))
    return query_grad, item_grad


def local(item_table, query_table, query_weight, query_ids, fetch_rows, counts, example_pos):
    table_rows, model_width = item_table.shape
    sources = fetch_rows.shape[1]
    slot_cap = fetch_rows.shape[2]
    scaling = model_width ** (-0.5)
    requests = fetch_rows.reshape(sources, slot_cap)
    wanted = lax.all_to_all(requests, ("batch", "table"), split_axis=0, concat_axis=0, tiled=True)
    found_rows = jnp.take(item_table, wanted, axis=0)
    fetched = lax.all_to_all(
        found_rows, ("batch", "table"), split_axis=0, concat_axis=0, tiled=True
    )
    slot_ids = slot_index(counts.reshape(sources), example_pos, slot_cap)
    item_vectors = jnp.take(fetched.reshape(sources * slot_cap, model_width), slot_ids, axis=0)
    looked = jnp.take(query_table, query_ids, axis=0).astype(jnp.float32)
    hidden = jnp.mean(looked, axis=1).astype(jnp.bfloat16)
    queries = jnp.dot(hidden, query_weight, preferred_element_type=jnp.float32).astype(jnp.bfloat16)
    side = int(round(lax.axis_size("batch") ** 0.5))
    if side * side == lax.axis_size("batch") and side > 1:
        query_grad, item_grad = block_grads(queries, item_vectors, "batch", side, scaling)
    else:
        group_queries = lax.all_gather(queries, "batch", axis=0, tiled=True)
        group_items = lax.all_gather(item_vectors, "batch", axis=0, tiled=True)
        query_grad, totals = forward(queries, group_items, item_vectors)
        side = int(round(lax.axis_size("batch") ** 0.5))
        if side * side == lax.axis_size("batch"):
            group_totals = plane_gather(totals[:, :1].reshape(1, -1), "batch", side)
        else:
            group_totals = lax.all_gather(totals[:, :1].reshape(1, -1), "batch", axis=1, tiled=True)
        scores_back = scaling * lax.dot_general(
            item_vectors, group_queries, (((1,), (1,)), ((), ())), preferred_element_type=jnp.float32
        )
        soft_back = jnp.exp(scores_back - group_totals).astype(jnp.bfloat16)
        summed = jnp.dot(soft_back, group_queries, preferred_element_type=jnp.float32)
        item_grad = scaling * (summed - queries.astype(jnp.float32))
    slot_grads = jax.ops.segment_sum(item_grad, slot_ids, num_segments=sources * slot_cap)
    slot_grads = slot_grads.reshape(sources, slot_cap, model_width)
    returned = lax.all_to_all(
        slot_grads, ("batch", "table"), split_axis=0, concat_axis=0, tiled=True
    )
    table_grad = (
        jnp.zeros((table_rows, model_width), jnp.float32)
        .at[wanted.reshape(-1)]
        .add(returned.reshape(-1, model_width))
    )
    partial_value = lax.dot_general(
        hidden,
        query_grad.astype(jnp.bfloat16),
        (((0,), (0,)), ((), ())),
        preferred_element_type=jnp.float32,
    )
    weight_grad = butterfly_sum(partial_value, ("batch", "table"))
    return (table_grad, weight_grad)


def solution(mesh):
    in_specs = (
        P(("batch", "table"), None),
        P(),
        P(),
        P(("batch", "table"), None),
        P(("batch", "table"), None, None),
        P(("batch", "table"), None),
        P(("batch", "table")),
    )
    out_specs = (P(("batch", "table"), None), P())
    return jax.shard_map(local, mesh=mesh, in_specs=in_specs, out_specs=out_specs, check_vma=False)
```

```python
import functools

import jax
import jax.numpy as jnp
from jax import lax
from jax.experimental import pallas as pl
from jax.experimental.pallas import tpu as pltpu
from jax.sharding import PartitionSpec as P


def forward_block(q_ref, items_ref, own_ref, grad_ref, totals_ref, *, scaling):
    scores = scaling * lax.dot_general(
        q_ref[...], items_ref[...], (((1,), (1,)), ((), ())), preferred_element_type=jnp.float32
    )
    highest = jnp.max(scores, axis=1, keepdims=True)
    totals = highest + jnp.log(jnp.sum(jnp.exp(scores - highest), axis=1, keepdims=True))
    soft_weights = jnp.exp(scores - totals).astype(jnp.bfloat16)
    pulled = jnp.dot(soft_weights, items_ref[...], preferred_element_type=jnp.float32)
    grad_ref[...] = scaling * (pulled - own_ref[...].astype(jnp.float32))
    totals_ref[...] = jnp.broadcast_to(totals, totals_ref.shape)


def forward(queries, group_items, item_vectors, tile=256):
    rows, width = queries.shape
    group = group_items.shape[0]
    return pl.pallas_call(
        functools.partial(forward_block, scaling=width ** (-0.5)),
        grid=(rows // tile,),
        in_specs=[
            pl.BlockSpec((tile, width), lambda i: (i, 0)),
            pl.BlockSpec((group, width), lambda i: (0, 0)),
            pl.BlockSpec((tile, width), lambda i: (i, 0)),
        ],
        out_specs=[
            pl.BlockSpec((tile, width), lambda i: (i, 0)),
            pl.BlockSpec((tile, 128), lambda i: (i, 0)),
        ],
        out_shape=[
            jax.ShapeDtypeStruct((rows, width), jnp.float32),
            jax.ShapeDtypeStruct((rows, 128), jnp.float32),
        ],
        compiler_params=pltpu.CompilerParams(vmem_limit_bytes=48 * 1024 * 1024),
    )(queries, group_items, item_vectors)


def plane_gather(value, axis, side):
    size = side * side
    index = lax.axis_index(axis)
    column = index % side
    line = index // side

    def shift(piece, step, along_row):
        pairs = []
        for source in range(size):
            high, low = divmod(source, side)
            if along_row:
                target = high * side + (low + step) % side
            else:
                target = ((high + step) % side) * side + low
            pairs.append((source, target))
        return lax.ppermute(piece, axis, pairs)

    pieces = jnp.stack([value] + [shift(value, step, True) for step in range(1, side)])
    row = jnp.concatenate([jnp.take(pieces, (column - c) % side, axis=0) for c in range(side)], axis=1)
    rows = jnp.stack([row] + [shift(row, step, False) for step in range(1, side)])
    return jnp.concatenate([jnp.take(rows, (line - r) % side, axis=0) for r in range(side)], axis=1)


def slot_index(live_slots, positions, slot_cap):
    ending = jnp.cumsum(live_slots)
    holder = jnp.sum((ending[None, :] <= positions[:, None]).astype(jnp.int32), axis=1)
    opening = ending - live_slots
    return holder * slot_cap + positions - jnp.take(opening, holder)


def butterfly_sum(value, axes):
    total = 1
    for axis in axes:
        total *= lax.axis_size(axis)
    step = 1
    while step < total:
        pairs = [(i, i ^ step) for i in range(total)]
        value = value + lax.ppermute(value, axes, pairs)
        step *= 2
    return value


def plane_shift(value, axis, side, step, along_row):
    pairs = []
    for source in range(side * side):
        high, low = divmod(source, side)
        if along_row:
            target = high * side + (low + step) % side
        else:
            target = ((high + step) % side) * side + low
        pairs.append((source, target))
    return lax.ppermute(value, axis, pairs)


def plane_gather_rows(value, axis, side, along_row):
    pieces = [value] + [plane_shift(value, axis, side, step, along_row) for step in range(1, side)]
    return jnp.concatenate(pieces, axis=0)


def plane_reduce_rows(value, axis, side, along_row):
    block = value.shape[0] // side
    total = value[:block]
    for step in range(1, side):
        part = value[((side - step) % side) * block:((side - step) % side + 1) * block]
        total = total + plane_shift(part, axis, side, step, along_row)
    return total


def block_grads(queries, item_vectors, axis, side, scaling):
    row_queries = plane_gather_rows(queries, axis, side, True)
    column_items = plane_gather_rows(item_vectors, axis, side, False)
    scores = scaling * lax.dot_general(
        row_queries, column_items, (((1,), (1,)), ((), ())), preferred_element_type=jnp.float32
    )
    local_max = jnp.max(scores, axis=1)
    local_sum = jnp.sum(jnp.exp(scores - local_max[:, None]), axis=1)
    stats = jnp.stack([local_max, local_sum])
    block = queries.shape[0]
    gathered = [stats] + [
        jnp.roll(plane_shift(stats, axis, side, step, True), step * block, axis=1) for step in range(1, side)
    ]
    highest = gathered[0][0]
    for other in gathered[1:]:
        highest = jnp.maximum(highest, other[0])
    mass = gathered[0][1] * jnp.exp(gathered[0][0] - highest)
    for other in gathered[1:]:
        mass = mass + other[1] * jnp.exp(other[0] - highest)
    totals = highest + jnp.log(mass)
    soft_weights = jnp.exp(scores - totals[:, None]).astype(jnp.bfloat16)
    pulled = jnp.dot(soft_weights, column_items, preferred_element_type=jnp.float32)
    pushed = lax.dot_general(
        soft_weights, row_queries, (((0,), (0,)), ((), ())), preferred_element_type=jnp.float32
    )
    pulled = plane_reduce_rows(pulled, axis, side, True)
    pushed = plane_reduce_rows(pushed, axis, side, False)
    query_grad = scaling * (pulled - item_vectors.astype(jnp.float32))
    item_grad = scaling * (pushed - queries.astype(jnp.float32))
    return query_grad, item_grad


def local(item_table, query_table, query_weight, query_ids, fetch_rows, counts, example_pos):
    table_rows, model_width = item_table.shape
    sources = fetch_rows.shape[1]
    slot_cap = fetch_rows.shape[2]
    scaling = model_width ** (-0.5)
    requests = fetch_rows.reshape(sources, slot_cap)
    wanted = lax.all_to_all(requests, ("batch", "table"), split_axis=0, concat_axis=0, tiled=True)
    found_rows = jnp.take(item_table, wanted, axis=0)
    found_rows, query_ids = lax.optimization_barrier((found_rows, query_ids))
    fetched = lax.all_to_all(
        found_rows, ("batch", "table"), split_axis=0, concat_axis=0, tiled=True
    )
    slot_ids = slot_index(counts.reshape(sources), example_pos, slot_cap)
    item_vectors = jnp.take(fetched.reshape(sources * slot_cap, model_width), slot_ids, axis=0)
    looked = jnp.take(query_table, query_ids, axis=0).astype(jnp.float32)
    hidden = jnp.mean(looked, axis=1).astype(jnp.bfloat16)
    queries = jnp.dot(hidden, query_weight, preferred_element_type=jnp.float32).astype(jnp.bfloat16)
    side = int(round(lax.axis_size("batch") ** 0.5))
    if side * side == lax.axis_size("batch") and side > 1:
        query_grad, item_grad = block_grads(queries, item_vectors, "batch", side, scaling)
    else:
        group_queries = lax.all_gather(queries, "batch", axis=0, tiled=True)
        group_items = lax.all_gather(item_vectors, "batch", axis=0, tiled=True)
        query_grad, totals = forward(queries, group_items, item_vectors)
        side = int(round(lax.axis_size("batch") ** 0.5))
        if side * side == lax.axis_size("batch"):
            group_totals = plane_gather(totals[:, :1].reshape(1, -1), "batch", side)
        else:
            group_totals = lax.all_gather(totals[:, :1].reshape(1, -1), "batch", axis=1, tiled=True)
        scores_back = scaling * lax.dot_general(
            item_vectors, group_queries, (((1,), (1,)), ((), ())), preferred_element_type=jnp.float32
        )
        soft_back = jnp.exp(scores_back - group_totals).astype(jnp.bfloat16)
        summed = jnp.dot(soft_back, group_queries, preferred_element_type=jnp.float32)
        item_grad = scaling * (summed - queries.astype(jnp.float32))
    slot_grads = jax.ops.segment_sum(item_grad, slot_ids, num_segments=sources * slot_cap)
    slot_grads = slot_grads.reshape(sources, slot_cap, model_width)
    returned = lax.all_to_all(
        slot_grads, ("batch", "table"), split_axis=0, concat_axis=0, tiled=True
    )
    table_grad = (
        jnp.zeros((table_rows, model_width), jnp.float32)
        .at[wanted.reshape(-1)]
        .add(returned.reshape(-1, model_width))
    )
    partial_value = lax.dot_general(
        hidden,
        query_grad.astype(jnp.bfloat16),
        (((0,), (0,)), ((), ())),
        preferred_element_type=jnp.float32,
    )
    weight_grad = butterfly_sum(partial_value, ("batch", "table"))
    return (table_grad, weight_grad)


def solution(mesh):
    in_specs = (
        P(("batch", "table"), None),
        P(),
        P(),
        P(("batch", "table"), None),
        P(("batch", "table"), None, None),
        P(("batch", "table"), None),
        P(("batch", "table")),
    )
    out_specs = (P(("batch", "table"), None), P())
    return jax.shard_map(local, mesh=mesh, in_specs=in_specs, out_specs=out_specs, check_vma=False)
```

```python
import functools

import jax
import jax.numpy as jnp
from jax import lax
from jax.experimental import pallas as pl
from jax.experimental.pallas import tpu as pltpu
from jax.sharding import PartitionSpec as P


def forward_block(q_ref, items_ref, own_ref, grad_ref, totals_ref, *, scaling):
    scores = scaling * lax.dot_general(
        q_ref[...], items_ref[...], (((1,), (1,)), ((), ())), preferred_element_type=jnp.float32
    )
    highest = jnp.max(scores, axis=1, keepdims=True)
    totals = highest + jnp.log(jnp.sum(jnp.exp(scores - highest), axis=1, keepdims=True))
    soft_weights = jnp.exp(scores - totals).astype(jnp.bfloat16)
    pulled = jnp.dot(soft_weights, items_ref[...], preferred_element_type=jnp.float32)
    grad_ref[...] = scaling * (pulled - own_ref[...].astype(jnp.float32))
    totals_ref[...] = jnp.broadcast_to(totals, totals_ref.shape)


def forward(queries, group_items, item_vectors, tile=256):
    rows, width = queries.shape
    group = group_items.shape[0]
    return pl.pallas_call(
        functools.partial(forward_block, scaling=width ** (-0.5)),
        grid=(rows // tile,),
        in_specs=[
            pl.BlockSpec((tile, width), lambda i: (i, 0)),
            pl.BlockSpec((group, width), lambda i: (0, 0)),
            pl.BlockSpec((tile, width), lambda i: (i, 0)),
        ],
        out_specs=[
            pl.BlockSpec((tile, width), lambda i: (i, 0)),
            pl.BlockSpec((tile, 128), lambda i: (i, 0)),
        ],
        out_shape=[
            jax.ShapeDtypeStruct((rows, width), jnp.float32),
            jax.ShapeDtypeStruct((rows, 128), jnp.float32),
        ],
        compiler_params=pltpu.CompilerParams(vmem_limit_bytes=48 * 1024 * 1024),
    )(queries, group_items, item_vectors)


def plane_gather(value, axis, side):
    size = side * side
    index = lax.axis_index(axis)
    column = index % side
    line = index // side

    def shift(piece, step, along_row):
        pairs = []
        for source in range(size):
            high, low = divmod(source, side)
            if along_row:
                target = high * side + (low + step) % side
            else:
                target = ((high + step) % side) * side + low
            pairs.append((source, target))
        return lax.ppermute(piece, axis, pairs)

    pieces = jnp.stack([value] + [shift(value, step, True) for step in range(1, side)])
    row = jnp.concatenate([jnp.take(pieces, (column - c) % side, axis=0) for c in range(side)], axis=1)
    rows = jnp.stack([row] + [shift(row, step, False) for step in range(1, side)])
    return jnp.concatenate([jnp.take(rows, (line - r) % side, axis=0) for r in range(side)], axis=1)


def slot_index(live_slots, positions, slot_cap):
    ending = jnp.cumsum(live_slots)
    holder = jnp.sum((ending[None, :] <= positions[:, None]).astype(jnp.int32), axis=1)
    opening = ending - live_slots
    return holder * slot_cap + positions - jnp.take(opening, holder)


def tree_sum(value, axes, inner):
    total = 1
    for axis in axes:
        total *= lax.axis_size(axis)
    index = 0
    for axis in axes:
        index = index * lax.axis_size(axis) + lax.axis_index(axis)
    step = 1
    while step < inner and step < total and value.shape[0] % 2 == 0:
        half = value.shape[0] // 2
        upper = (index & step) != 0
        keep = jnp.where(upper, value[half:], value[:half])
        send = jnp.where(upper, value[:half], value[half:])
        value = keep + lax.ppermute(send, axes, [(i, i ^ step) for i in range(total)])
        step *= 2
    halved = step
    while step < total:
        value = value + lax.ppermute(value, axes, [(i, i ^ step) for i in range(total)])
        step *= 2
    step = halved // 2
    while step >= 1:
        got = lax.ppermute(value, axes, [(i, i ^ step) for i in range(total)])
        upper = (index & step) != 0
        value = jnp.where(upper, jnp.concatenate([got, value]), jnp.concatenate([value, got]))
        step //= 2
    return value


def butterfly_sum(value, axes):
    total = 1
    for axis in axes:
        total *= lax.axis_size(axis)
    step = 1
    while step < total:
        pairs = [(i, i ^ step) for i in range(total)]
        value = value + lax.ppermute(value, axes, pairs)
        step *= 2
    return value


def plane_shift(value, axis, side, step, along_row):
    pairs = []
    for source in range(side * side):
        high, low = divmod(source, side)
        if along_row:
            target = high * side + (low + step) % side
        else:
            target = ((high + step) % side) * side + low
        pairs.append((source, target))
    return lax.ppermute(value, axis, pairs)


def plane_gather_rows(value, axis, side, along_row):
    pieces = [value] + [plane_shift(value, axis, side, step, along_row) for step in range(1, side)]
    return jnp.concatenate(pieces, axis=0)


def plane_reduce_rows(value, axis, side, along_row):
    block = value.shape[0] // side
    total = value[:block]
    for step in range(1, side):
        part = value[((side - step) % side) * block:((side - step) % side + 1) * block]
        total = total + plane_shift(part, axis, side, step, along_row)
    return total


def block_grads(queries, item_vectors, axis, side, scaling):
    row_queries = plane_gather_rows(queries, axis, side, True)
    column_items = plane_gather_rows(item_vectors, axis, side, False)
    scores = scaling * lax.dot_general(
        row_queries, column_items, (((1,), (1,)), ((), ())), preferred_element_type=jnp.float32
    )
    local_max = jnp.max(scores, axis=1)
    local_sum = jnp.sum(jnp.exp(scores - local_max[:, None]), axis=1)
    stats = jnp.stack([local_max, local_sum])
    block = queries.shape[0]
    gathered = [stats] + [
        jnp.roll(plane_shift(stats, axis, side, step, True), step * block, axis=1) for step in range(1, side)
    ]
    highest = gathered[0][0]
    for other in gathered[1:]:
        highest = jnp.maximum(highest, other[0])
    mass = gathered[0][1] * jnp.exp(gathered[0][0] - highest)
    for other in gathered[1:]:
        mass = mass + other[1] * jnp.exp(other[0] - highest)
    totals = highest + jnp.log(mass)
    soft_weights = jnp.exp(scores - totals[:, None]).astype(jnp.bfloat16)
    pulled = jnp.dot(soft_weights, column_items, preferred_element_type=jnp.float32)
    pushed = lax.dot_general(
        soft_weights, row_queries, (((0,), (0,)), ((), ())), preferred_element_type=jnp.float32
    )
    pulled, pushed = lax.optimization_barrier((pulled, pushed))
    pulled = plane_reduce_rows(pulled, axis, side, True)
    pushed = plane_reduce_rows(pushed, axis, side, False)
    query_grad = scaling * (pulled - item_vectors.astype(jnp.float32))
    item_grad = scaling * (pushed - queries.astype(jnp.float32))
    return query_grad, item_grad


def local(item_table, query_table, query_weight, query_ids, fetch_rows, counts, example_pos):
    table_rows, model_width = item_table.shape
    sources = fetch_rows.shape[1]
    slot_cap = fetch_rows.shape[2]
    scaling = model_width ** (-0.5)
    requests = fetch_rows.reshape(sources, slot_cap)
    wanted = lax.all_to_all(requests, ("batch", "table"), split_axis=0, concat_axis=0, tiled=True)
    found_rows = jnp.take(item_table, wanted, axis=0)
    found_rows, query_ids = lax.optimization_barrier((found_rows, query_ids))
    fetched = lax.all_to_all(
        found_rows, ("batch", "table"), split_axis=0, concat_axis=0, tiled=True
    )
    slot_ids = slot_index(counts.reshape(sources), example_pos, slot_cap)
    item_vectors = jnp.take(fetched.reshape(sources * slot_cap, model_width), slot_ids, axis=0)
    looked = jnp.take(query_table, query_ids, axis=0).astype(jnp.float32)
    hidden = jnp.mean(looked, axis=1).astype(jnp.bfloat16)
    queries = jnp.dot(hidden, query_weight, preferred_element_type=jnp.float32).astype(jnp.bfloat16)
    side = int(round(lax.axis_size("batch") ** 0.5))
    if side * side == lax.axis_size("batch") and side > 1:
        query_grad, item_grad = block_grads(queries, item_vectors, "batch", side, scaling)
    else:
        group_queries = lax.all_gather(queries, "batch", axis=0, tiled=True)
        group_items = lax.all_gather(item_vectors, "batch", axis=0, tiled=True)
        query_grad, totals = forward(queries, group_items, item_vectors)
        side = int(round(lax.axis_size("batch") ** 0.5))
        if side * side == lax.axis_size("batch"):
            group_totals = plane_gather(totals[:, :1].reshape(1, -1), "batch", side)
        else:
            group_totals = lax.all_gather(totals[:, :1].reshape(1, -1), "batch", axis=1, tiled=True)
        scores_back = scaling * lax.dot_general(
            item_vectors, group_queries, (((1,), (1,)), ((), ())), preferred_element_type=jnp.float32
        )
        soft_back = jnp.exp(scores_back - group_totals).astype(jnp.bfloat16)
        summed = jnp.dot(soft_back, group_queries, preferred_element_type=jnp.float32)
        item_grad = scaling * (summed - queries.astype(jnp.float32))
    slot_grads = jax.ops.segment_sum(item_grad, slot_ids, num_segments=sources * slot_cap)
    slot_grads = slot_grads.reshape(sources, slot_cap, model_width)
    returned = lax.all_to_all(
        slot_grads, ("batch", "table"), split_axis=0, concat_axis=0, tiled=True
    )
    table_grad = (
        jnp.zeros((table_rows, model_width), jnp.float32)
        .at[wanted.reshape(-1)]
        .add(returned.reshape(-1, model_width))
    )
    partial_value = lax.dot_general(
        hidden,
        query_grad.astype(jnp.bfloat16),
        (((0,), (0,)), ((), ())),
        preferred_element_type=jnp.float32,
    )
    total = lax.axis_size("batch") * lax.axis_size("table")
    if total & (total - 1) == 0:
        weight_grad = tree_sum(partial_value, ("batch", "table"), min(8, lax.axis_size("table")))
    else:
        weight_grad = lax.psum(partial_value, ("batch", "table"))
    return (table_grad, weight_grad)


def solution(mesh):
    in_specs = (
        P(("batch", "table"), None),
        P(),
        P(),
        P(("batch", "table"), None),
        P(("batch", "table"), None, None),
        P(("batch", "table"), None),
        P(("batch", "table")),
    )
    out_specs = (P(("batch", "table"), None), P())
    return jax.shard_map(local, mesh=mesh, in_specs=in_specs, out_specs=out_specs, check_vma=False)
```

```python
import functools

import jax
import jax.numpy as jnp
from jax import lax
from jax.experimental import pallas as pl
from jax.experimental.pallas import tpu as pltpu
from jax.sharding import PartitionSpec as P


def forward_block(q_ref, items_ref, own_ref, grad_ref, totals_ref, *, scaling):
    scores = scaling * lax.dot_general(
        q_ref[...], items_ref[...], (((1,), (1,)), ((), ())), preferred_element_type=jnp.float32
    )
    highest = jnp.max(scores, axis=1, keepdims=True)
    totals = highest + jnp.log(jnp.sum(jnp.exp(scores - highest), axis=1, keepdims=True))
    soft_weights = jnp.exp(scores - totals).astype(jnp.bfloat16)
    pulled = jnp.dot(soft_weights, items_ref[...], preferred_element_type=jnp.float32)
    grad_ref[...] = scaling * (pulled - own_ref[...].astype(jnp.float32))
    totals_ref[...] = jnp.broadcast_to(totals, totals_ref.shape)


def forward(queries, group_items, item_vectors, tile=256):
    rows, width = queries.shape
    group = group_items.shape[0]
    return pl.pallas_call(
        functools.partial(forward_block, scaling=width ** (-0.5)),
        grid=(rows // tile,),
        in_specs=[
            pl.BlockSpec((tile, width), lambda i: (i, 0)),
            pl.BlockSpec((group, width), lambda i: (0, 0)),
            pl.BlockSpec((tile, width), lambda i: (i, 0)),
        ],
        out_specs=[
            pl.BlockSpec((tile, width), lambda i: (i, 0)),
            pl.BlockSpec((tile, 128), lambda i: (i, 0)),
        ],
        out_shape=[
            jax.ShapeDtypeStruct((rows, width), jnp.float32),
            jax.ShapeDtypeStruct((rows, 128), jnp.float32),
        ],
        compiler_params=pltpu.CompilerParams(vmem_limit_bytes=48 * 1024 * 1024),
    )(queries, group_items, item_vectors)


def plane_gather(value, axis, side):
    size = side * side
    index = lax.axis_index(axis)
    column = index % side
    line = index // side

    def shift(piece, step, along_row):
        pairs = []
        for source in range(size):
            high, low = divmod(source, side)
            if along_row:
                target = high * side + (low + step) % side
            else:
                target = ((high + step) % side) * side + low
            pairs.append((source, target))
        return lax.ppermute(piece, axis, pairs)

    pieces = jnp.stack([value] + [shift(value, step, True) for step in range(1, side)])
    row = jnp.concatenate([jnp.take(pieces, (column - c) % side, axis=0) for c in range(side)], axis=1)
    rows = jnp.stack([row] + [shift(row, step, False) for step in range(1, side)])
    return jnp.concatenate([jnp.take(rows, (line - r) % side, axis=0) for r in range(side)], axis=1)


def slot_index(live_slots, positions, slot_cap):
    ending = jnp.cumsum(live_slots)
    holder = jnp.sum((ending[None, :] <= positions[:, None]).astype(jnp.int32), axis=1)
    opening = ending - live_slots
    return holder * slot_cap + positions - jnp.take(opening, holder)


def tree_sum(value, axes, inner):
    total = 1
    for axis in axes:
        total *= lax.axis_size(axis)
    index = 0
    for axis in axes:
        index = index * lax.axis_size(axis) + lax.axis_index(axis)
    step = 1
    while step < inner and step < total and value.shape[0] % 2 == 0:
        half = value.shape[0] // 2
        upper = (index & step) != 0
        keep = jnp.where(upper, value[half:], value[:half])
        send = jnp.where(upper, value[:half], value[half:])
        value = keep + lax.ppermute(send, axes, [(i, i ^ step) for i in range(total)])
        step *= 2
    halved = step
    while step < total:
        value = value + lax.ppermute(value, axes, [(i, i ^ step) for i in range(total)])
        step *= 2
    step = halved // 2
    while step >= 1:
        got = lax.ppermute(value, axes, [(i, i ^ step) for i in range(total)])
        upper = (index & step) != 0
        value = jnp.where(upper, jnp.concatenate([got, value]), jnp.concatenate([value, got]))
        step //= 2
    return value


def butterfly_sum(value, axes):
    total = 1
    for axis in axes:
        total *= lax.axis_size(axis)
    step = 1
    while step < total:
        pairs = [(i, i ^ step) for i in range(total)]
        value = value + lax.ppermute(value, axes, pairs)
        step *= 2
    return value


def plane_shift(value, axis, side, step, along_row):
    pairs = []
    for source in range(side * side):
        high, low = divmod(source, side)
        if along_row:
            target = high * side + (low + step) % side
        else:
            target = ((high + step) % side) * side + low
        pairs.append((source, target))
    return lax.ppermute(value, axis, pairs)


def plane_gather_rows(value, axis, side, along_row):
    pieces = [value] + [plane_shift(value, axis, side, step, along_row) for step in range(1, side)]
    return jnp.concatenate(pieces, axis=0)


def plane_reduce_rows(value, axis, side, along_row):
    block = value.shape[0] // side
    total = value[:block]
    for step in range(1, side):
        part = value[((side - step) % side) * block:((side - step) % side + 1) * block]
        total = total + plane_shift(part, axis, side, step, along_row)
    return total


def block_grads(hidden, query_weight, item_vectors, axis, side, scaling):
    row_hidden = plane_gather_rows(hidden, axis, side, True)
    column_items = plane_gather_rows(item_vectors, axis, side, False)
    row_queries = jnp.dot(row_hidden, query_weight, preferred_element_type=jnp.float32).astype(jnp.bfloat16)
    scores = scaling * lax.dot_general(
        row_queries, column_items, (((1,), (1,)), ((), ())), preferred_element_type=jnp.float32
    )
    local_max = jnp.max(scores, axis=1)
    local_sum = jnp.sum(jnp.exp(scores - local_max[:, None]), axis=1)
    stats = jnp.stack([local_max, local_sum])
    block = hidden.shape[0]
    gathered = [stats] + [
        jnp.roll(plane_shift(stats, axis, side, step, True), step * block, axis=1) for step in range(1, side)
    ]
    highest = gathered[0][0]
    for other in gathered[1:]:
        highest = jnp.maximum(highest, other[0])
    mass = gathered[0][1] * jnp.exp(gathered[0][0] - highest)
    for other in gathered[1:]:
        mass = mass + other[1] * jnp.exp(other[0] - highest)
    totals = highest + jnp.log(mass)
    soft_weights = jnp.exp(scores - totals[:, None]).astype(jnp.bfloat16)
    pulled = jnp.dot(soft_weights, column_items, preferred_element_type=jnp.float32)
    pushed = lax.dot_general(
        soft_weights, row_queries, (((0,), (0,)), ((), ())), preferred_element_type=jnp.float32
    )
    weight_part = lax.dot_general(
        row_hidden, pulled, (((0,), (0,)), ((), ())),
        preferred_element_type=jnp.float32, precision=lax.Precision.HIGHEST,
    ) - lax.dot_general(
        hidden, item_vectors, (((0,), (0,)), ((), ())), preferred_element_type=jnp.float32
    )
    pushed = plane_reduce_rows(pushed, axis, side, False)
    item_grad = scaling * (pushed - row_queries[:block].astype(jnp.float32))
    return item_grad, scaling * weight_part


def local(item_table, query_table, query_weight, query_ids, fetch_rows, counts, example_pos):
    table_rows, model_width = item_table.shape
    sources = fetch_rows.shape[1]
    slot_cap = fetch_rows.shape[2]
    scaling = model_width ** (-0.5)
    requests = fetch_rows.reshape(sources, slot_cap)
    wanted = lax.all_to_all(requests, ("batch", "table"), split_axis=0, concat_axis=0, tiled=True)
    found_rows = jnp.take(item_table, wanted, axis=0)
    found_rows, query_ids = lax.optimization_barrier((found_rows, query_ids))
    fetched = lax.all_to_all(
        found_rows, ("batch", "table"), split_axis=0, concat_axis=0, tiled=True
    )
    slot_ids = slot_index(counts.reshape(sources), example_pos, slot_cap)
    item_vectors = jnp.take(fetched.reshape(sources * slot_cap, model_width), slot_ids, axis=0)
    looked = jnp.take(query_table, query_ids, axis=0).astype(jnp.float32)
    hidden = jnp.mean(looked, axis=1).astype(jnp.bfloat16)
    queries = jnp.dot(hidden, query_weight, preferred_element_type=jnp.float32).astype(jnp.bfloat16)
    side = int(round(lax.axis_size("batch") ** 0.5))
    if side * side == lax.axis_size("batch") and side > 1:
        item_grad, partial_value = block_grads(hidden, query_weight, item_vectors, "batch", side, scaling)
    else:
        group_queries = lax.all_gather(queries, "batch", axis=0, tiled=True)
        group_items = lax.all_gather(item_vectors, "batch", axis=0, tiled=True)
        query_grad, totals = forward(queries, group_items, item_vectors)
        side = int(round(lax.axis_size("batch") ** 0.5))
        if side * side == lax.axis_size("batch"):
            group_totals = plane_gather(totals[:, :1].reshape(1, -1), "batch", side)
        else:
            group_totals = lax.all_gather(totals[:, :1].reshape(1, -1), "batch", axis=1, tiled=True)
        scores_back = scaling * lax.dot_general(
            item_vectors, group_queries, (((1,), (1,)), ((), ())), preferred_element_type=jnp.float32
        )
        soft_back = jnp.exp(scores_back - group_totals).astype(jnp.bfloat16)
        summed = jnp.dot(soft_back, group_queries, preferred_element_type=jnp.float32)
        item_grad = scaling * (summed - queries.astype(jnp.float32))
        partial_value = lax.dot_general(
            hidden,
            query_grad.astype(jnp.bfloat16),
            (((0,), (0,)), ((), ())),
            preferred_element_type=jnp.float32,
        )
    slot_grads = jax.ops.segment_sum(item_grad, slot_ids, num_segments=sources * slot_cap)
    slot_grads = slot_grads.reshape(sources, slot_cap, model_width)
    returned = lax.all_to_all(
        slot_grads, ("batch", "table"), split_axis=0, concat_axis=0, tiled=True
    )
    table_grad = (
        jnp.zeros((table_rows, model_width), jnp.float32)
        .at[wanted.reshape(-1)]
        .add(returned.reshape(-1, model_width))
    )
    total = lax.axis_size("batch") * lax.axis_size("table")
    if total & (total - 1) == 0:
        weight_grad = tree_sum(partial_value, ("batch", "table"), min(8, lax.axis_size("table")))
    else:
        weight_grad = lax.psum(partial_value, ("batch", "table"))
    return (table_grad, weight_grad)


def solution(mesh):
    in_specs = (
        P(("batch", "table"), None),
        P(),
        P(),
        P(("batch", "table"), None),
        P(("batch", "table"), None, None),
        P(("batch", "table"), None),
        P(("batch", "table")),
    )
    out_specs = (P(("batch", "table"), None), P())
    return jax.shard_map(local, mesh=mesh, in_specs=in_specs, out_specs=out_specs, check_vma=False)
```

```python
import functools

import jax
import jax.numpy as jnp
from jax import lax
from jax.experimental import pallas as pl
from jax.experimental.pallas import tpu as pltpu
from jax.sharding import PartitionSpec as P


def forward_block(q_ref, items_ref, own_ref, grad_ref, totals_ref, *, scaling):
    scores = scaling * lax.dot_general(
        q_ref[...], items_ref[...], (((1,), (1,)), ((), ())), preferred_element_type=jnp.float32
    )
    highest = jnp.max(scores, axis=1, keepdims=True)
    totals = highest + jnp.log(jnp.sum(jnp.exp(scores - highest), axis=1, keepdims=True))
    soft_weights = jnp.exp(scores - totals).astype(jnp.bfloat16)
    pulled = jnp.dot(soft_weights, items_ref[...], preferred_element_type=jnp.float32)
    grad_ref[...] = scaling * (pulled - own_ref[...].astype(jnp.float32))
    totals_ref[...] = jnp.broadcast_to(totals, totals_ref.shape)


def forward(queries, group_items, item_vectors, tile=256):
    rows, width = queries.shape
    group = group_items.shape[0]
    return pl.pallas_call(
        functools.partial(forward_block, scaling=width ** (-0.5)),
        grid=(rows // tile,),
        in_specs=[
            pl.BlockSpec((tile, width), lambda i: (i, 0)),
            pl.BlockSpec((group, width), lambda i: (0, 0)),
            pl.BlockSpec((tile, width), lambda i: (i, 0)),
        ],
        out_specs=[
            pl.BlockSpec((tile, width), lambda i: (i, 0)),
            pl.BlockSpec((tile, 128), lambda i: (i, 0)),
        ],
        out_shape=[
            jax.ShapeDtypeStruct((rows, width), jnp.float32),
            jax.ShapeDtypeStruct((rows, 128), jnp.float32),
        ],
        compiler_params=pltpu.CompilerParams(vmem_limit_bytes=48 * 1024 * 1024),
    )(queries, group_items, item_vectors)


def plane_gather(value, axis, side):
    size = side * side
    index = lax.axis_index(axis)
    column = index % side
    line = index // side

    def shift(piece, step, along_row):
        pairs = []
        for source in range(size):
            high, low = divmod(source, side)
            if along_row:
                target = high * side + (low + step) % side
            else:
                target = ((high + step) % side) * side + low
            pairs.append((source, target))
        return lax.ppermute(piece, axis, pairs)

    pieces = jnp.stack([value] + [shift(value, step, True) for step in range(1, side)])
    row = jnp.concatenate([jnp.take(pieces, (column - c) % side, axis=0) for c in range(side)], axis=1)
    rows = jnp.stack([row] + [shift(row, step, False) for step in range(1, side)])
    return jnp.concatenate([jnp.take(rows, (line - r) % side, axis=0) for r in range(side)], axis=1)


def slot_index(live_slots, positions, slot_cap):
    ending = jnp.cumsum(live_slots)
    holder = jnp.sum((ending[None, :] <= positions[:, None]).astype(jnp.int32), axis=1)
    opening = ending - live_slots
    return holder * slot_cap + positions - jnp.take(opening, holder)


def tree_sum(value, axes, inner):
    total = 1
    for axis in axes:
        total *= lax.axis_size(axis)
    index = 0
    for axis in axes:
        index = index * lax.axis_size(axis) + lax.axis_index(axis)
    step = 1
    while step < inner and step < total and value.shape[0] % 2 == 0:
        half = value.shape[0] // 2
        upper = (index & step) != 0
        keep = jnp.where(upper, value[half:], value[:half])
        send = jnp.where(upper, value[:half], value[half:])
        value = keep + lax.ppermute(send, axes, [(i, i ^ step) for i in range(total)])
        step *= 2
    halved = step
    while step < total:
        value = value + lax.ppermute(value, axes, [(i, i ^ step) for i in range(total)])
        step *= 2
    step = halved // 2
    while step >= 1:
        got = lax.ppermute(value, axes, [(i, i ^ step) for i in range(total)])
        upper = (index & step) != 0
        value = jnp.where(upper, jnp.concatenate([got, value]), jnp.concatenate([value, got]))
        step //= 2
    return value


def butterfly_sum(value, axes):
    total = 1
    for axis in axes:
        total *= lax.axis_size(axis)
    step = 1
    while step < total:
        pairs = [(i, i ^ step) for i in range(total)]
        value = value + lax.ppermute(value, axes, pairs)
        step *= 2
    return value


def plane_shift(value, axis, side, step, along_row):
    pairs = []
    for source in range(side * side):
        high, low = divmod(source, side)
        if along_row:
            target = high * side + (low + step) % side
        else:
            target = ((high + step) % side) * side + low
        pairs.append((source, target))
    return lax.ppermute(value, axis, pairs)


def plane_gather_rows(value, axis, side, along_row):
    pieces = [value] + [plane_shift(value, axis, side, step, along_row) for step in range(1, side)]
    return jnp.concatenate(pieces, axis=0)


def plane_reduce_rows(value, axis, side, along_row):
    block = value.shape[0] // side
    total = value[:block]
    for step in range(1, side):
        part = value[((side - step) % side) * block:((side - step) % side + 1) * block]
        total = total + plane_shift(part, axis, side, step, along_row)
    return total


def block_grads(hidden, query_weight, item_vectors, axis, side, scaling):
    row_hidden = plane_gather_rows(hidden, axis, side, True)
    column_items = plane_gather_rows(item_vectors, axis, side, False)
    row_queries = jnp.dot(row_hidden, query_weight, preferred_element_type=jnp.float32).astype(jnp.bfloat16)
    scores = scaling * lax.dot_general(
        row_queries, column_items, (((1,), (1,)), ((), ())), preferred_element_type=jnp.float32
    )
    local_max = jnp.max(scores, axis=1)
    local_sum = jnp.sum(jnp.exp(scores - local_max[:, None]), axis=1)
    stats = jnp.stack([local_max, local_sum])
    block = hidden.shape[0]
    gathered = [stats] + [
        jnp.roll(plane_shift(stats, axis, side, step, True), step * block, axis=1) for step in range(1, side)
    ]
    highest = gathered[0][0]
    for other in gathered[1:]:
        highest = jnp.maximum(highest, other[0])
    mass = gathered[0][1] * jnp.exp(gathered[0][0] - highest)
    for other in gathered[1:]:
        mass = mass + other[1] * jnp.exp(other[0] - highest)
    totals = highest + jnp.log(mass)
    soft_weights = jnp.exp(scores - totals[:, None]).astype(jnp.bfloat16)
    pulled = jnp.dot(soft_weights, column_items, preferred_element_type=jnp.float32)
    pushed = lax.dot_general(
        soft_weights, row_queries, (((0,), (0,)), ((), ())), preferred_element_type=jnp.float32
    )
    weight_part = lax.dot_general(
        row_hidden, pulled, (((0,), (0,)), ((), ())),
        preferred_element_type=jnp.float32, precision=lax.Precision.HIGHEST,
    ) - lax.dot_general(
        hidden, item_vectors, (((0,), (0,)), ((), ())), preferred_element_type=jnp.float32
    )
    pushed = plane_reduce_rows(pushed, axis, side, False)
    item_grad = scaling * (pushed - row_queries[:block].astype(jnp.float32))
    return item_grad, scaling * weight_part


def local(item_table, query_table, query_weight, query_ids, fetch_rows, counts, example_pos):
    table_rows, model_width = item_table.shape
    sources = fetch_rows.shape[1]
    slot_cap = fetch_rows.shape[2]
    scaling = model_width ** (-0.5)
    requests = fetch_rows.reshape(sources, slot_cap)
    wanted = lax.all_to_all(requests, ("batch", "table"), split_axis=0, concat_axis=0, tiled=True)
    found_rows = jnp.take(item_table, wanted, axis=0)
    found_rows, query_ids = lax.optimization_barrier((found_rows, query_ids))
    fetched = lax.all_to_all(
        found_rows, ("batch", "table"), split_axis=0, concat_axis=0, tiled=True
    )
    slot_ids = slot_index(counts.reshape(sources), example_pos, slot_cap)
    item_vectors = jnp.take(fetched.reshape(sources * slot_cap, model_width), slot_ids, axis=0)
    looked = jnp.take(query_table, query_ids, axis=0).astype(jnp.float32)
    hidden = jnp.mean(looked, axis=1).astype(jnp.bfloat16)
    queries = jnp.dot(hidden, query_weight, preferred_element_type=jnp.float32).astype(jnp.bfloat16)
    side = int(round(lax.axis_size("batch") ** 0.5))
    if side * side == lax.axis_size("batch") and side > 1:
        item_grad, partial_value = block_grads(hidden, query_weight, item_vectors, "batch", side, scaling)
    else:
        group_queries = lax.all_gather(queries, "batch", axis=0, tiled=True)
        group_items = lax.all_gather(item_vectors, "batch", axis=0, tiled=True)
        query_grad, totals = forward(queries, group_items, item_vectors)
        side = int(round(lax.axis_size("batch") ** 0.5))
        if side * side == lax.axis_size("batch"):
            group_totals = plane_gather(totals[:, :1].reshape(1, -1), "batch", side)
        else:
            group_totals = lax.all_gather(totals[:, :1].reshape(1, -1), "batch", axis=1, tiled=True)
        scores_back = scaling * lax.dot_general(
            item_vectors, group_queries, (((1,), (1,)), ((), ())), preferred_element_type=jnp.float32
        )
        soft_back = jnp.exp(scores_back - group_totals).astype(jnp.bfloat16)
        summed = jnp.dot(soft_back, group_queries, preferred_element_type=jnp.float32)
        item_grad = scaling * (summed - queries.astype(jnp.float32))
        partial_value = lax.dot_general(
            hidden,
            query_grad.astype(jnp.bfloat16),
            (((0,), (0,)), ((), ())),
            preferred_element_type=jnp.float32,
        )
    total = lax.axis_size("batch") * lax.axis_size("table")
    if total & (total - 1) == 0:
        weight_grad = tree_sum(partial_value, ("batch", "table"), min(8, lax.axis_size("table")))
    else:
        weight_grad = lax.psum(partial_value, ("batch", "table"))
    item_grad, weight_grad = lax.optimization_barrier((item_grad, weight_grad))
    slot_grads = jax.ops.segment_sum(item_grad, slot_ids, num_segments=sources * slot_cap)
    slot_grads = slot_grads.reshape(sources, slot_cap, model_width)
    returned = lax.all_to_all(
        slot_grads, ("batch", "table"), split_axis=0, concat_axis=0, tiled=True
    )
    table_grad = (
        jnp.zeros((table_rows, model_width), jnp.float32)
        .at[wanted.reshape(-1)]
        .add(returned.reshape(-1, model_width))
    )
    return (table_grad, weight_grad)


def solution(mesh):
    in_specs = (
        P(("batch", "table"), None),
        P(),
        P(),
        P(("batch", "table"), None),
        P(("batch", "table"), None, None),
        P(("batch", "table"), None),
        P(("batch", "table")),
    )
    out_specs = (P(("batch", "table"), None), P())
    return jax.shard_map(local, mesh=mesh, in_specs=in_specs, out_specs=out_specs, check_vma=False)
```

```python
import functools

import jax
import jax.numpy as jnp
from jax import lax
from jax.experimental import pallas as pl
from jax.experimental.pallas import tpu as pltpu
from jax.sharding import PartitionSpec as P


def forward_block(q_ref, items_ref, own_ref, grad_ref, totals_ref, *, scaling):
    scores = scaling * lax.dot_general(
        q_ref[...], items_ref[...], (((1,), (1,)), ((), ())), preferred_element_type=jnp.float32
    )
    highest = jnp.max(scores, axis=1, keepdims=True)
    totals = highest + jnp.log(jnp.sum(jnp.exp(scores - highest), axis=1, keepdims=True))
    soft_weights = jnp.exp(scores - totals).astype(jnp.bfloat16)
    pulled = jnp.dot(soft_weights, items_ref[...], preferred_element_type=jnp.float32)
    grad_ref[...] = scaling * (pulled - own_ref[...].astype(jnp.float32))
    totals_ref[...] = jnp.broadcast_to(totals, totals_ref.shape)


def forward(queries, group_items, item_vectors, tile=256):
    rows, width = queries.shape
    group = group_items.shape[0]
    return pl.pallas_call(
        functools.partial(forward_block, scaling=width ** (-0.5)),
        grid=(rows // tile,),
        in_specs=[
            pl.BlockSpec((tile, width), lambda i: (i, 0)),
            pl.BlockSpec((group, width), lambda i: (0, 0)),
            pl.BlockSpec((tile, width), lambda i: (i, 0)),
        ],
        out_specs=[
            pl.BlockSpec((tile, width), lambda i: (i, 0)),
            pl.BlockSpec((tile, 128), lambda i: (i, 0)),
        ],
        out_shape=[
            jax.ShapeDtypeStruct((rows, width), jnp.float32),
            jax.ShapeDtypeStruct((rows, 128), jnp.float32),
        ],
        compiler_params=pltpu.CompilerParams(vmem_limit_bytes=48 * 1024 * 1024),
    )(queries, group_items, item_vectors)


def stats_block(q_ref, items_ref, stats_ref, *, scaling):
    scores = scaling * lax.dot_general(q_ref[...], items_ref[...], (((1,), (1,)), ((), ())), preferred_element_type=jnp.float32)
    highest = jnp.max(scores, axis=1, keepdims=True)
    mass = jnp.sum(jnp.exp(scores - highest), axis=1, keepdims=True)
    lane = lax.broadcasted_iota(jnp.int32, stats_ref.shape, 1)
    stats_ref[...] = jnp.where(lane == 0, highest, mass)

def block_stats(queries, items, scaling, tile=256):
    rows, width = queries.shape
    return pl.pallas_call(
        functools.partial(stats_block, scaling=scaling),
        grid=(rows // tile,),
        in_specs=[pl.BlockSpec((tile, width), lambda i: (i, 0)), pl.BlockSpec(items.shape, lambda i: (0, 0))],
        out_specs=pl.BlockSpec((tile, 128), lambda i: (i, 0)),
        out_shape=jax.ShapeDtypeStruct((rows, 128), jnp.float32),
        compiler_params=pltpu.CompilerParams(vmem_limit_bytes=48 * 1024 * 1024),
    )(queries, items)

def grads_block(q_ref, items_ref, totals_ref, pulled_ref, pushed_ref, *, scaling):
    scores = scaling * lax.dot_general(q_ref[...], items_ref[...], (((1,), (1,)), ((), ())), preferred_element_type=jnp.float32)
    soft = jnp.exp(scores - totals_ref[:, :1]).astype(jnp.bfloat16)
    pulled_ref[...] = jnp.dot(soft, items_ref[...], preferred_element_type=jnp.float32)
    part = lax.dot_general(soft, q_ref[...], (((0,), (0,)), ((), ())), preferred_element_type=jnp.float32)
    @pl.when(pl.program_id(0) == 0)
    def _():
        pushed_ref[...] = part
    @pl.when(pl.program_id(0) != 0)
    def _():
        pushed_ref[...] += part

def block_grads_k(queries, items, totals, scaling, tile=256):
    rows, width = queries.shape
    return pl.pallas_call(
        functools.partial(grads_block, scaling=scaling),
        grid=(rows // tile,),
        in_specs=[pl.BlockSpec((tile, width), lambda i: (i, 0)), pl.BlockSpec(items.shape, lambda i: (0, 0)),
                  pl.BlockSpec((tile, 128), lambda i: (i, 0))],
        out_specs=[pl.BlockSpec((tile, width), lambda i: (i, 0)), pl.BlockSpec((items.shape[0], width), lambda i: (0, 0))],
        out_shape=[jax.ShapeDtypeStruct((rows, width), jnp.float32), jax.ShapeDtypeStruct((items.shape[0], width), jnp.float32)],
        compiler_params=pltpu.CompilerParams(vmem_limit_bytes=48 * 1024 * 1024, dimension_semantics=("arbitrary",)),
    )(queries, items, totals)

def plane_gather(value, axis, side):
    size = side * side
    index = lax.axis_index(axis)
    column = index % side
    line = index // side

    def shift(piece, step, along_row):
        pairs = []
        for source in range(size):
            high, low = divmod(source, side)
            if along_row:
                target = high * side + (low + step) % side
            else:
                target = ((high + step) % side) * side + low
            pairs.append((source, target))
        return lax.ppermute(piece, axis, pairs)

    pieces = jnp.stack([value] + [shift(value, step, True) for step in range(1, side)])
    row = jnp.concatenate([jnp.take(pieces, (column - c) % side, axis=0) for c in range(side)], axis=1)
    rows = jnp.stack([row] + [shift(row, step, False) for step in range(1, side)])
    return jnp.concatenate([jnp.take(rows, (line - r) % side, axis=0) for r in range(side)], axis=1)


def slot_index(live_slots, positions, slot_cap):
    ending = jnp.cumsum(live_slots)
    holder = jnp.sum((ending[None, :] <= positions[:, None]).astype(jnp.int32), axis=1)
    opening = ending - live_slots
    return holder * slot_cap + positions - jnp.take(opening, holder)


def tree_sum(value, axes, inner):
    total = 1
    for axis in axes:
        total *= lax.axis_size(axis)
    index = 0
    for axis in axes:
        index = index * lax.axis_size(axis) + lax.axis_index(axis)
    step = 1
    while step < inner and step < total and value.shape[0] % 2 == 0:
        half = value.shape[0] // 2
        upper = (index & step) != 0
        keep = jnp.where(upper, value[half:], value[:half])
        send = jnp.where(upper, value[:half], value[half:])
        value = keep + lax.ppermute(send, axes, [(i, i ^ step) for i in range(total)])
        step *= 2
    halved = step
    while step < total:
        value = value + lax.ppermute(value, axes, [(i, i ^ step) for i in range(total)])
        step *= 2
    step = halved // 2
    while step >= 1:
        got = lax.ppermute(value, axes, [(i, i ^ step) for i in range(total)])
        upper = (index & step) != 0
        value = jnp.where(upper, jnp.concatenate([got, value]), jnp.concatenate([value, got]))
        step //= 2
    return value


def butterfly_sum(value, axes):
    total = 1
    for axis in axes:
        total *= lax.axis_size(axis)
    step = 1
    while step < total:
        pairs = [(i, i ^ step) for i in range(total)]
        value = value + lax.ppermute(value, axes, pairs)
        step *= 2
    return value


def plane_shift(value, axis, side, step, along_row):
    pairs = []
    for source in range(side * side):
        high, low = divmod(source, side)
        if along_row:
            target = high * side + (low + step) % side
        else:
            target = ((high + step) % side) * side + low
        pairs.append((source, target))
    return lax.ppermute(value, axis, pairs)


def plane_gather_rows(value, axis, side, along_row):
    pieces = [value] + [plane_shift(value, axis, side, step, along_row) for step in range(1, side)]
    return jnp.concatenate(pieces, axis=0)


def plane_reduce_rows(value, axis, side, along_row):
    block = value.shape[0] // side
    total = value[:block]
    for step in range(1, side):
        part = value[((side - step) % side) * block:((side - step) % side + 1) * block]
        total = total + plane_shift(part, axis, side, step, along_row)
    return total


def block_grads(hidden, query_weight, item_vectors, axis, side, scaling):
    row_hidden = plane_gather_rows(hidden, axis, side, True)
    column_items = plane_gather_rows(item_vectors, axis, side, False)
    row_queries = jnp.dot(row_hidden, query_weight, preferred_element_type=jnp.float32).astype(jnp.bfloat16)
    stats = block_stats(row_queries, column_items, scaling)
    local_max = stats[:, 0]
    local_sum = stats[:, 1]
    stats = jnp.stack([local_max, local_sum])
    block = hidden.shape[0]
    gathered = [stats] + [
        jnp.roll(plane_shift(stats, axis, side, step, True), step * block, axis=1) for step in range(1, side)
    ]
    highest = gathered[0][0]
    for other in gathered[1:]:
        highest = jnp.maximum(highest, other[0])
    mass = gathered[0][1] * jnp.exp(gathered[0][0] - highest)
    for other in gathered[1:]:
        mass = mass + other[1] * jnp.exp(other[0] - highest)
    totals = highest + jnp.log(mass)
    lanes = jnp.broadcast_to(totals[:, None], (totals.shape[0], 128))
    pulled, pushed = block_grads_k(row_queries, column_items, lanes, scaling)
    weight_part = lax.dot_general(
        row_hidden, pulled, (((0,), (0,)), ((), ())),
        preferred_element_type=jnp.float32, precision=lax.Precision.HIGHEST,
    ) - lax.dot_general(
        hidden, item_vectors, (((0,), (0,)), ((), ())), preferred_element_type=jnp.float32
    )
    pushed = plane_reduce_rows(pushed, axis, side, False)
    item_grad = scaling * (pushed - row_queries[:block].astype(jnp.float32))
    return item_grad, scaling * weight_part


def local(item_table, query_table, query_weight, query_ids, fetch_rows, counts, example_pos):
    table_rows, model_width = item_table.shape
    sources = fetch_rows.shape[1]
    slot_cap = fetch_rows.shape[2]
    scaling = model_width ** (-0.5)
    requests = fetch_rows.reshape(sources, slot_cap)
    wanted = lax.all_to_all(requests, ("batch", "table"), split_axis=0, concat_axis=0, tiled=True)
    found_rows = jnp.take(item_table, wanted, axis=0)
    found_rows, query_ids = lax.optimization_barrier((found_rows, query_ids))
    fetched = lax.all_to_all(
        found_rows, ("batch", "table"), split_axis=0, concat_axis=0, tiled=True
    )
    slot_ids = slot_index(counts.reshape(sources), example_pos, slot_cap)
    item_vectors = jnp.take(fetched.reshape(sources * slot_cap, model_width), slot_ids, axis=0)
    looked = jnp.take(query_table, query_ids, axis=0).astype(jnp.float32)
    hidden = jnp.mean(looked, axis=1).astype(jnp.bfloat16)
    queries = jnp.dot(hidden, query_weight, preferred_element_type=jnp.float32).astype(jnp.bfloat16)
    side = int(round(lax.axis_size("batch") ** 0.5))
    if side * side == lax.axis_size("batch") and side > 1:
        item_grad, partial_value = block_grads(hidden, query_weight, item_vectors, "batch", side, scaling)
    else:
        group_queries = lax.all_gather(queries, "batch", axis=0, tiled=True)
        group_items = lax.all_gather(item_vectors, "batch", axis=0, tiled=True)
        query_grad, totals = forward(queries, group_items, item_vectors)
        side = int(round(lax.axis_size("batch") ** 0.5))
        if side * side == lax.axis_size("batch"):
            group_totals = plane_gather(totals[:, :1].reshape(1, -1), "batch", side)
        else:
            group_totals = lax.all_gather(totals[:, :1].reshape(1, -1), "batch", axis=1, tiled=True)
        scores_back = scaling * lax.dot_general(
            item_vectors, group_queries, (((1,), (1,)), ((), ())), preferred_element_type=jnp.float32
        )
        soft_back = jnp.exp(scores_back - group_totals).astype(jnp.bfloat16)
        summed = jnp.dot(soft_back, group_queries, preferred_element_type=jnp.float32)
        item_grad = scaling * (summed - queries.astype(jnp.float32))
        partial_value = lax.dot_general(
            hidden,
            query_grad.astype(jnp.bfloat16),
            (((0,), (0,)), ((), ())),
            preferred_element_type=jnp.float32,
        )
    total = lax.axis_size("batch") * lax.axis_size("table")
    if total & (total - 1) == 0:
        weight_grad = tree_sum(partial_value, ("batch", "table"), min(8, lax.axis_size("table")))
    else:
        weight_grad = lax.psum(partial_value, ("batch", "table"))
    item_grad, weight_grad = lax.optimization_barrier((item_grad, weight_grad))
    slot_grads = jax.ops.segment_sum(item_grad, slot_ids, num_segments=sources * slot_cap)
    slot_grads = slot_grads.reshape(sources, slot_cap, model_width)
    returned = lax.all_to_all(
        slot_grads, ("batch", "table"), split_axis=0, concat_axis=0, tiled=True
    )
    table_grad = (
        jnp.zeros((table_rows, model_width), jnp.float32)
        .at[wanted.reshape(-1)]
        .add(returned.reshape(-1, model_width))
    )
    return (table_grad, weight_grad)


def solution(mesh):
    in_specs = (
        P(("batch", "table"), None),
        P(),
        P(),
        P(("batch", "table"), None),
        P(("batch", "table"), None, None),
        P(("batch", "table"), None),
        P(("batch", "table")),
    )
    out_specs = (P(("batch", "table"), None), P())
    return jax.shard_map(local, mesh=mesh, in_specs=in_specs, out_specs=out_specs, check_vma=False)
```

```python
import functools

import jax
import jax.numpy as jnp
from jax import lax
from jax.experimental import pallas as pl
from jax.experimental.pallas import tpu as pltpu
from jax.sharding import PartitionSpec as P


def forward_block(q_ref, items_ref, own_ref, grad_ref, totals_ref, *, scaling):
    scores = scaling * lax.dot_general(
        q_ref[...], items_ref[...], (((1,), (1,)), ((), ())), preferred_element_type=jnp.float32
    )
    highest = jnp.max(scores, axis=1, keepdims=True)
    totals = highest + jnp.log(jnp.sum(jnp.exp(scores - highest), axis=1, keepdims=True))
    soft_weights = jnp.exp(scores - totals).astype(jnp.bfloat16)
    pulled = jnp.dot(soft_weights, items_ref[...], preferred_element_type=jnp.float32)
    grad_ref[...] = scaling * (pulled - own_ref[...].astype(jnp.float32))
    totals_ref[...] = jnp.broadcast_to(totals, totals_ref.shape)


def forward(queries, group_items, item_vectors, tile=256):
    rows, width = queries.shape
    group = group_items.shape[0]
    return pl.pallas_call(
        functools.partial(forward_block, scaling=width ** (-0.5)),
        grid=(rows // tile,),
        in_specs=[
            pl.BlockSpec((tile, width), lambda i: (i, 0)),
            pl.BlockSpec((group, width), lambda i: (0, 0)),
            pl.BlockSpec((tile, width), lambda i: (i, 0)),
        ],
        out_specs=[
            pl.BlockSpec((tile, width), lambda i: (i, 0)),
            pl.BlockSpec((tile, 128), lambda i: (i, 0)),
        ],
        out_shape=[
            jax.ShapeDtypeStruct((rows, width), jnp.float32),
            jax.ShapeDtypeStruct((rows, 128), jnp.float32),
        ],
        compiler_params=pltpu.CompilerParams(vmem_limit_bytes=48 * 1024 * 1024),
    )(queries, group_items, item_vectors)


def stats_block(q_ref, items_ref, stats_ref, *, scaling):
    scores = scaling * lax.dot_general(
        items_ref[...], q_ref[...], (((1,), (1,)), ((), ())), preferred_element_type=jnp.float32
    )
    highest = jnp.max(scores, axis=0, keepdims=True)
    stats_ref[0:1, :] = highest
    stats_ref[1:2, :] = jnp.sum(jnp.exp(scores - highest), axis=0, keepdims=True)


def block_stats(queries, items, scaling, tile=256):
    rows, width = queries.shape
    return pl.pallas_call(
        functools.partial(stats_block, scaling=scaling),
        grid=(rows // tile,),
        in_specs=[pl.BlockSpec((tile, width), lambda i: (i, 0)), pl.BlockSpec(items.shape, lambda i: (0, 0))],
        out_specs=pl.BlockSpec((2, tile), lambda i: (0, i)),
        out_shape=jax.ShapeDtypeStruct((2, rows), jnp.float32),
        compiler_params=pltpu.CompilerParams(vmem_limit_bytes=48 * 1024 * 1024),
    )(queries, items)


def grads_block(q_ref, items_ref, totals_ref, pulled_ref, pushed_ref, *, scaling):
    scores = scaling * lax.dot_general(
        items_ref[...], q_ref[...], (((1,), (1,)), ((), ())), preferred_element_type=jnp.float32
    )
    soft = jnp.exp(scores - totals_ref[...]).astype(jnp.bfloat16)
    pulled_ref[...] = lax.dot_general(
        soft, items_ref[...], (((0,), (0,)), ((), ())), preferred_element_type=jnp.float32
    )
    part = jnp.dot(soft, q_ref[...], preferred_element_type=jnp.float32)

    @pl.when(pl.program_id(0) == 0)
    def _():
        pushed_ref[...] = part

    @pl.when(pl.program_id(0) != 0)
    def _():
        pushed_ref[...] += part


def block_grads_k(queries, items, totals, scaling, tile=256):
    rows, width = queries.shape
    return pl.pallas_call(
        functools.partial(grads_block, scaling=scaling),
        grid=(rows // tile,),
        in_specs=[
            pl.BlockSpec((tile, width), lambda i: (i, 0)),
            pl.BlockSpec(items.shape, lambda i: (0, 0)),
            pl.BlockSpec((1, tile), lambda i: (0, i)),
        ],
        out_specs=[
            pl.BlockSpec((tile, width), lambda i: (i, 0)),
            pl.BlockSpec((items.shape[0], width), lambda i: (0, 0)),
        ],
        out_shape=[
            jax.ShapeDtypeStruct((rows, width), jnp.float32),
            jax.ShapeDtypeStruct((items.shape[0], width), jnp.float32),
        ],
        compiler_params=pltpu.CompilerParams(
            vmem_limit_bytes=48 * 1024 * 1024, dimension_semantics=("arbitrary",)
        ),
    )(queries, items, totals)


def plane_gather(value, axis, side):
    size = side * side
    index = lax.axis_index(axis)
    column = index % side
    line = index // side

    def shift(piece, step, along_row):
        pairs = []
        for source in range(size):
            high, low = divmod(source, side)
            if along_row:
                target = high * side + (low + step) % side
            else:
                target = ((high + step) % side) * side + low
            pairs.append((source, target))
        return lax.ppermute(piece, axis, pairs)

    pieces = jnp.stack([value] + [shift(value, step, True) for step in range(1, side)])
    row = jnp.concatenate([jnp.take(pieces, (column - c) % side, axis=0) for c in range(side)], axis=1)
    rows = jnp.stack([row] + [shift(row, step, False) for step in range(1, side)])
    return jnp.concatenate([jnp.take(rows, (line - r) % side, axis=0) for r in range(side)], axis=1)


def slot_index(live_slots, positions, slot_cap):
    ending = jnp.cumsum(live_slots)
    holder = jnp.sum((ending[None, :] <= positions[:, None]).astype(jnp.int32), axis=1)
    opening = ending - live_slots
    return holder * slot_cap + positions - jnp.take(opening, holder)


def tree_sum(value, axes, inner):
    total = 1
    for axis in axes:
        total *= lax.axis_size(axis)
    index = 0
    for axis in axes:
        index = index * lax.axis_size(axis) + lax.axis_index(axis)
    step = 1
    while step < inner and step < total and value.shape[0] % 2 == 0:
        half = value.shape[0] // 2
        upper = (index & step) != 0
        keep = jnp.where(upper, value[half:], value[:half])
        send = jnp.where(upper, value[:half], value[half:])
        value = keep + lax.ppermute(send, axes, [(i, i ^ step) for i in range(total)])
        step *= 2
    halved = step
    while step < total:
        value = value + lax.ppermute(value, axes, [(i, i ^ step) for i in range(total)])
        step *= 2
    step = halved // 2
    while step >= 1:
        got = lax.ppermute(value, axes, [(i, i ^ step) for i in range(total)])
        upper = (index & step) != 0
        value = jnp.where(upper, jnp.concatenate([got, value]), jnp.concatenate([value, got]))
        step //= 2
    return value


def butterfly_sum(value, axes):
    total = 1
    for axis in axes:
        total *= lax.axis_size(axis)
    step = 1
    while step < total:
        pairs = [(i, i ^ step) for i in range(total)]
        value = value + lax.ppermute(value, axes, pairs)
        step *= 2
    return value


def plane_shift(value, axis, side, step, along_row):
    pairs = []
    for source in range(side * side):
        high, low = divmod(source, side)
        if along_row:
            target = high * side + (low + step) % side
        else:
            target = ((high + step) % side) * side + low
        pairs.append((source, target))
    return lax.ppermute(value, axis, pairs)


def plane_gather_rows(value, axis, side, along_row):
    pieces = [value] + [plane_shift(value, axis, side, step, along_row) for step in range(1, side)]
    return jnp.concatenate(pieces, axis=0)


def plane_reduce_rows(value, axis, side, along_row):
    block = value.shape[0] // side
    total = value[:block]
    for step in range(1, side):
        part = value[((side - step) % side) * block:((side - step) % side + 1) * block]
        total = total + plane_shift(part, axis, side, step, along_row)
    return total


def block_grads(hidden, query_weight, item_vectors, axis, side, scaling):
    row_hidden = plane_gather_rows(hidden, axis, side, True)
    column_items = plane_gather_rows(item_vectors, axis, side, False)
    row_queries = jnp.dot(row_hidden, query_weight, preferred_element_type=jnp.float32).astype(jnp.bfloat16)
    stats = block_stats(row_queries, column_items, scaling)
    block = hidden.shape[0]
    gathered = [stats] + [
        jnp.roll(plane_shift(stats, axis, side, step, True), step * block, axis=1) for step in range(1, side)
    ]
    highest = gathered[0][0]
    for other in gathered[1:]:
        highest = jnp.maximum(highest, other[0])
    mass = gathered[0][1] * jnp.exp(gathered[0][0] - highest)
    for other in gathered[1:]:
        mass = mass + other[1] * jnp.exp(other[0] - highest)
    totals = highest + jnp.log(mass)
    pulled, pushed = block_grads_k(row_queries, column_items, totals.reshape(1, -1), scaling)
    weight_part = lax.dot_general(
        row_hidden, pulled, (((0,), (0,)), ((), ())),
        preferred_element_type=jnp.float32, precision=lax.Precision.HIGHEST,
    ) - lax.dot_general(
        hidden, item_vectors, (((0,), (0,)), ((), ())), preferred_element_type=jnp.float32
    )
    pushed = plane_reduce_rows(pushed, axis, side, False)
    item_grad = scaling * (pushed - row_queries[:block].astype(jnp.float32))
    return item_grad, scaling * weight_part


def local(item_table, query_table, query_weight, query_ids, fetch_rows, counts, example_pos):
    table_rows, model_width = item_table.shape
    sources = fetch_rows.shape[1]
    slot_cap = fetch_rows.shape[2]
    scaling = model_width ** (-0.5)
    requests = fetch_rows.reshape(sources, slot_cap)
    wanted = lax.all_to_all(requests, ("batch", "table"), split_axis=0, concat_axis=0, tiled=True)
    found_rows = jnp.take(item_table, wanted, axis=0)
    found_rows, query_ids = lax.optimization_barrier((found_rows, query_ids))
    fetched = lax.all_to_all(
        found_rows, ("batch", "table"), split_axis=0, concat_axis=0, tiled=True
    )
    slot_ids = slot_index(counts.reshape(sources), example_pos, slot_cap)
    item_vectors = jnp.take(fetched.reshape(sources * slot_cap, model_width), slot_ids, axis=0)
    looked = jnp.take(query_table, query_ids, axis=0).astype(jnp.float32)
    hidden = jnp.mean(looked, axis=1).astype(jnp.bfloat16)
    queries = jnp.dot(hidden, query_weight, preferred_element_type=jnp.float32).astype(jnp.bfloat16)
    side = int(round(lax.axis_size("batch") ** 0.5))
    if side * side == lax.axis_size("batch") and side > 1:
        item_grad, partial_value = block_grads(hidden, query_weight, item_vectors, "batch", side, scaling)
    else:
        group_queries = lax.all_gather(queries, "batch", axis=0, tiled=True)
        group_items = lax.all_gather(item_vectors, "batch", axis=0, tiled=True)
        query_grad, totals = forward(queries, group_items, item_vectors)
        side = int(round(lax.axis_size("batch") ** 0.5))
        if side * side == lax.axis_size("batch"):
            group_totals = plane_gather(totals[:, :1].reshape(1, -1), "batch", side)
        else:
            group_totals = lax.all_gather(totals[:, :1].reshape(1, -1), "batch", axis=1, tiled=True)
        scores_back = scaling * lax.dot_general(
            item_vectors, group_queries, (((1,), (1,)), ((), ())), preferred_element_type=jnp.float32
        )
        soft_back = jnp.exp(scores_back - group_totals).astype(jnp.bfloat16)
        summed = jnp.dot(soft_back, group_queries, preferred_element_type=jnp.float32)
        item_grad = scaling * (summed - queries.astype(jnp.float32))
        partial_value = lax.dot_general(
            hidden,
            query_grad.astype(jnp.bfloat16),
            (((0,), (0,)), ((), ())),
            preferred_element_type=jnp.float32,
        )
    total = lax.axis_size("batch") * lax.axis_size("table")
    if total & (total - 1) == 0:
        weight_grad = tree_sum(partial_value, ("batch", "table"), min(8, lax.axis_size("table")))
    else:
        weight_grad = lax.psum(partial_value, ("batch", "table"))
    item_grad, weight_grad = lax.optimization_barrier((item_grad, weight_grad))
    slot_grads = jax.ops.segment_sum(item_grad, slot_ids, num_segments=sources * slot_cap)
    slot_grads = slot_grads.reshape(sources, slot_cap, model_width)
    returned = lax.all_to_all(
        slot_grads, ("batch", "table"), split_axis=0, concat_axis=0, tiled=True
    )
    table_grad = (
        jnp.zeros((table_rows, model_width), jnp.float32)
        .at[wanted.reshape(-1)]
        .add(returned.reshape(-1, model_width))
    )
    return (table_grad, weight_grad)


def solution(mesh):
    in_specs = (
        P(("batch", "table"), None),
        P(),
        P(),
        P(("batch", "table"), None),
        P(("batch", "table"), None, None),
        P(("batch", "table"), None),
        P(("batch", "table")),
    )
    out_specs = (P(("batch", "table"), None), P())
    return jax.shard_map(local, mesh=mesh, in_specs=in_specs, out_specs=out_specs, check_vma=False)
```

```python
import functools

import jax
import jax.numpy as jnp
from jax import lax
from jax.experimental import pallas as pl
from jax.experimental.pallas import tpu as pltpu
from jax.sharding import PartitionSpec as P


def forward_block(q_ref, items_ref, own_ref, grad_ref, totals_ref, *, scaling):
    scores = scaling * lax.dot_general(
        q_ref[...], items_ref[...], (((1,), (1,)), ((), ())), preferred_element_type=jnp.float32
    )
    highest = jnp.max(scores, axis=1, keepdims=True)
    totals = highest + jnp.log(jnp.sum(jnp.exp(scores - highest), axis=1, keepdims=True))
    soft_weights = jnp.exp(scores - totals).astype(jnp.bfloat16)
    pulled = jnp.dot(soft_weights, items_ref[...], preferred_element_type=jnp.float32)
    grad_ref[...] = scaling * (pulled - own_ref[...].astype(jnp.float32))
    totals_ref[...] = jnp.broadcast_to(totals, totals_ref.shape)


def forward(queries, group_items, item_vectors, tile=256):
    rows, width = queries.shape
    group = group_items.shape[0]
    return pl.pallas_call(
        functools.partial(forward_block, scaling=width ** (-0.5)),
        grid=(rows // tile,),
        in_specs=[
            pl.BlockSpec((tile, width), lambda i: (i, 0)),
            pl.BlockSpec((group, width), lambda i: (0, 0)),
            pl.BlockSpec((tile, width), lambda i: (i, 0)),
        ],
        out_specs=[
            pl.BlockSpec((tile, width), lambda i: (i, 0)),
            pl.BlockSpec((tile, 128), lambda i: (i, 0)),
        ],
        out_shape=[
            jax.ShapeDtypeStruct((rows, width), jnp.float32),
            jax.ShapeDtypeStruct((rows, 128), jnp.float32),
        ],
        compiler_params=pltpu.CompilerParams(vmem_limit_bytes=48 * 1024 * 1024),
    )(queries, group_items, item_vectors)


def stats_block(q_ref, items_ref, stats_ref, *, scaling):
    scores = scaling * lax.dot_general(
        items_ref[...], q_ref[...], (((1,), (1,)), ((), ())), preferred_element_type=jnp.float32
    )
    highest = jnp.max(scores, axis=0, keepdims=True)
    stats_ref[0:1, :] = highest
    stats_ref[1:2, :] = jnp.sum(jnp.exp(scores - highest), axis=0, keepdims=True)


def block_stats(queries, items, scaling, tile=256):
    rows, width = queries.shape
    return pl.pallas_call(
        functools.partial(stats_block, scaling=scaling),
        grid=(rows // tile,),
        in_specs=[pl.BlockSpec((tile, width), lambda i: (i, 0)), pl.BlockSpec(items.shape, lambda i: (0, 0))],
        out_specs=pl.BlockSpec((2, tile), lambda i: (0, i)),
        out_shape=jax.ShapeDtypeStruct((2, rows), jnp.float32),
        compiler_params=pltpu.CompilerParams(vmem_limit_bytes=48 * 1024 * 1024),
    )(queries, items)


def grads_block(q_ref, items_ref, totals_ref, pulled_ref, pushed_ref, *, scaling):
    scores = scaling * lax.dot_general(
        items_ref[...], q_ref[...], (((1,), (1,)), ((), ())), preferred_element_type=jnp.float32
    )
    soft = jnp.exp(scores - totals_ref[...]).astype(jnp.bfloat16)
    pulled_ref[...] = lax.dot_general(
        soft, items_ref[...], (((0,), (0,)), ((), ())), preferred_element_type=jnp.float32
    )
    part = jnp.dot(soft, q_ref[...], preferred_element_type=jnp.float32)

    @pl.when(pl.program_id(0) == 0)
    def _():
        pushed_ref[...] = part

    @pl.when(pl.program_id(0) != 0)
    def _():
        pushed_ref[...] += part


def block_grads_k(queries, items, totals, scaling, tile=256):
    rows, width = queries.shape
    return pl.pallas_call(
        functools.partial(grads_block, scaling=scaling),
        grid=(rows // tile,),
        in_specs=[
            pl.BlockSpec((tile, width), lambda i: (i, 0)),
            pl.BlockSpec(items.shape, lambda i: (0, 0)),
            pl.BlockSpec((1, tile), lambda i: (0, i)),
        ],
        out_specs=[
            pl.BlockSpec((tile, width), lambda i: (i, 0)),
            pl.BlockSpec((items.shape[0], width), lambda i: (0, 0)),
        ],
        out_shape=[
            jax.ShapeDtypeStruct((rows, width), jnp.float32),
            jax.ShapeDtypeStruct((items.shape[0], width), jnp.float32),
        ],
        compiler_params=pltpu.CompilerParams(
            vmem_limit_bytes=48 * 1024 * 1024, dimension_semantics=("arbitrary",)
        ),
    )(queries, items, totals)


def plane_gather(value, axis, side):
    size = side * side
    index = lax.axis_index(axis)
    column = index % side
    line = index // side

    def shift(piece, step, along_row):
        pairs = []
        for source in range(size):
            high, low = divmod(source, side)
            if along_row:
                target = high * side + (low + step) % side
            else:
                target = ((high + step) % side) * side + low
            pairs.append((source, target))
        return lax.ppermute(piece, axis, pairs)

    pieces = jnp.stack([value] + [shift(value, step, True) for step in range(1, side)])
    row = jnp.concatenate([jnp.take(pieces, (column - c) % side, axis=0) for c in range(side)], axis=1)
    rows = jnp.stack([row] + [shift(row, step, False) for step in range(1, side)])
    return jnp.concatenate([jnp.take(rows, (line - r) % side, axis=0) for r in range(side)], axis=1)


def slot_index(live_slots, positions, slot_cap):
    ending = jnp.cumsum(live_slots)
    holder = jnp.sum((ending[None, :] <= positions[:, None]).astype(jnp.int32), axis=1)
    opening = ending - live_slots
    return holder * slot_cap + positions - jnp.take(opening, holder)


def flat_index(axes):
    total = 1
    index = 0
    for axis in axes:
        total *= lax.axis_size(axis)
        index = index * lax.axis_size(axis) + lax.axis_index(axis)
    return total, index


def tree_halve(value, axes, inner):
    total, index = flat_index(axes)
    step = 1
    while step < inner and step < total and value.shape[0] % 2 == 0:
        half = value.shape[0] // 2
        upper = (index & step) != 0
        keep = jnp.where(upper, value[half:], value[:half])
        send = jnp.where(upper, value[:half], value[half:])
        value = keep + lax.ppermute(send, axes, [(i, i ^ step) for i in range(total)])
        step *= 2
    return value, step


def tree_finish(value, axes, halved):
    total, index = flat_index(axes)
    step = halved
    while step < total:
        value = value + lax.ppermute(value, axes, [(i, i ^ step) for i in range(total)])
        step *= 2
    step = halved // 2
    while step >= 1:
        got = lax.ppermute(value, axes, [(i, i ^ step) for i in range(total)])
        upper = (index & step) != 0
        value = jnp.where(upper, jnp.concatenate([got, value]), jnp.concatenate([value, got]))
        step //= 2
    return value


def butterfly_sum(value, axes):
    total = 1
    for axis in axes:
        total *= lax.axis_size(axis)
    step = 1
    while step < total:
        pairs = [(i, i ^ step) for i in range(total)]
        value = value + lax.ppermute(value, axes, pairs)
        step *= 2
    return value


def plane_shift(value, axis, side, step, along_row):
    pairs = []
    for source in range(side * side):
        high, low = divmod(source, side)
        if along_row:
            target = high * side + (low + step) % side
        else:
            target = ((high + step) % side) * side + low
        pairs.append((source, target))
    return lax.ppermute(value, axis, pairs)


def plane_gather_rows(value, axis, side, along_row):
    pieces = [value] + [plane_shift(value, axis, side, step, along_row) for step in range(1, side)]
    return jnp.concatenate(pieces, axis=0)


def plane_reduce_rows(value, axis, side, along_row):
    block = value.shape[0] // side
    total = value[:block]
    for step in range(1, side):
        part = value[((side - step) % side) * block:((side - step) % side + 1) * block]
        total = total + plane_shift(part, axis, side, step, along_row)
    return total


def block_grads(hidden, query_weight, item_vectors, axis, side, scaling):
    row_hidden = plane_gather_rows(hidden, axis, side, True)
    column_items = plane_gather_rows(item_vectors, axis, side, False)
    row_queries = jnp.dot(row_hidden, query_weight, preferred_element_type=jnp.float32).astype(jnp.bfloat16)
    stats = block_stats(row_queries, column_items, scaling)
    block = hidden.shape[0]
    gathered = [stats] + [
        jnp.roll(plane_shift(stats, axis, side, step, True), step * block, axis=1) for step in range(1, side)
    ]
    highest = gathered[0][0]
    for other in gathered[1:]:
        highest = jnp.maximum(highest, other[0])
    mass = gathered[0][1] * jnp.exp(gathered[0][0] - highest)
    for other in gathered[1:]:
        mass = mass + other[1] * jnp.exp(other[0] - highest)
    totals = highest + jnp.log(mass)
    pulled, pushed = block_grads_k(row_queries, column_items, totals.reshape(1, -1), scaling)
    weight_part = lax.dot_general(
        row_hidden, pulled, (((0,), (0,)), ((), ())),
        preferred_element_type=jnp.float32, precision=lax.Precision.HIGHEST,
    ) - lax.dot_general(
        hidden, item_vectors, (((0,), (0,)), ((), ())), preferred_element_type=jnp.float32
    )
    pushed = plane_reduce_rows(pushed, axis, side, False)
    item_grad = scaling * (pushed - row_queries[:block].astype(jnp.float32))
    return item_grad, scaling * weight_part


def local(item_table, query_table, query_weight, query_ids, fetch_rows, counts, example_pos):
    table_rows, model_width = item_table.shape
    sources = fetch_rows.shape[1]
    slot_cap = fetch_rows.shape[2]
    scaling = model_width ** (-0.5)
    requests = fetch_rows.reshape(sources, slot_cap)
    wanted = lax.all_to_all(requests, ("batch", "table"), split_axis=0, concat_axis=0, tiled=True)
    found_rows = jnp.take(item_table, wanted, axis=0)
    found_rows, query_ids = lax.optimization_barrier((found_rows, query_ids))
    fetched = lax.all_to_all(
        found_rows, ("batch", "table"), split_axis=0, concat_axis=0, tiled=True
    )
    slot_ids = slot_index(counts.reshape(sources), example_pos, slot_cap)
    item_vectors = jnp.take(fetched.reshape(sources * slot_cap, model_width), slot_ids, axis=0)
    looked = jnp.take(query_table, query_ids, axis=0).astype(jnp.float32)
    hidden = jnp.mean(looked, axis=1).astype(jnp.bfloat16)
    queries = jnp.dot(hidden, query_weight, preferred_element_type=jnp.float32).astype(jnp.bfloat16)
    side = int(round(lax.axis_size("batch") ** 0.5))
    if side * side == lax.axis_size("batch") and side > 1:
        item_grad, partial_value = block_grads(hidden, query_weight, item_vectors, "batch", side, scaling)
    else:
        group_queries = lax.all_gather(queries, "batch", axis=0, tiled=True)
        group_items = lax.all_gather(item_vectors, "batch", axis=0, tiled=True)
        query_grad, totals = forward(queries, group_items, item_vectors)
        side = int(round(lax.axis_size("batch") ** 0.5))
        if side * side == lax.axis_size("batch"):
            group_totals = plane_gather(totals[:, :1].reshape(1, -1), "batch", side)
        else:
            group_totals = lax.all_gather(totals[:, :1].reshape(1, -1), "batch", axis=1, tiled=True)
        scores_back = scaling * lax.dot_general(
            item_vectors, group_queries, (((1,), (1,)), ((), ())), preferred_element_type=jnp.float32
        )
        soft_back = jnp.exp(scores_back - group_totals).astype(jnp.bfloat16)
        summed = jnp.dot(soft_back, group_queries, preferred_element_type=jnp.float32)
        item_grad = scaling * (summed - queries.astype(jnp.float32))
        partial_value = lax.dot_general(
            hidden,
            query_grad.astype(jnp.bfloat16),
            (((0,), (0,)), ((), ())),
            preferred_element_type=jnp.float32,
        )
    total = lax.axis_size("batch") * lax.axis_size("table")
    if total & (total - 1) == 0:
        shard, halved = tree_halve(partial_value, ("batch", "table"), min(8, lax.axis_size("table")))
        item_grad, shard = lax.optimization_barrier((item_grad, shard))
        weight_grad = tree_finish(shard, ("batch", "table"), halved)
    else:
        weight_grad = lax.psum(partial_value, ("batch", "table"))
    slot_grads = jax.ops.segment_sum(item_grad, slot_ids, num_segments=sources * slot_cap)
    slot_grads = slot_grads.reshape(sources, slot_cap, model_width)
    returned = lax.all_to_all(
        slot_grads, ("batch", "table"), split_axis=0, concat_axis=0, tiled=True
    )
    table_grad = (
        jnp.zeros((table_rows, model_width), jnp.float32)
        .at[wanted.reshape(-1)]
        .add(returned.reshape(-1, model_width))
    )
    return (table_grad, weight_grad)


def solution(mesh):
    in_specs = (
        P(("batch", "table"), None),
        P(),
        P(),
        P(("batch", "table"), None),
        P(("batch", "table"), None, None),
        P(("batch", "table"), None),
        P(("batch", "table")),
    )
    out_specs = (P(("batch", "table"), None), P())
    return jax.shard_map(local, mesh=mesh, in_specs=in_specs, out_specs=out_specs, check_vma=False)
```

```python
import functools

import jax
import jax.numpy as jnp
from jax import lax
from jax.experimental import pallas as pl
from jax.experimental.pallas import tpu as pltpu
from jax.sharding import PartitionSpec as P


def forward_block(q_ref, items_ref, own_ref, grad_ref, totals_ref, *, scaling):
    scores = scaling * lax.dot_general(
        q_ref[...], items_ref[...], (((1,), (1,)), ((), ())), preferred_element_type=jnp.float32
    )
    highest = jnp.max(scores, axis=1, keepdims=True)
    totals = highest + jnp.log(jnp.sum(jnp.exp(scores - highest), axis=1, keepdims=True))
    soft_weights = jnp.exp(scores - totals).astype(jnp.bfloat16)
    pulled = jnp.dot(soft_weights, items_ref[...], preferred_element_type=jnp.float32)
    grad_ref[...] = scaling * (pulled - own_ref[...].astype(jnp.float32))
    totals_ref[...] = jnp.broadcast_to(totals, totals_ref.shape)


def forward(queries, group_items, item_vectors, tile=256):
    rows, width = queries.shape
    group = group_items.shape[0]
    return pl.pallas_call(
        functools.partial(forward_block, scaling=width ** (-0.5)),
        grid=(rows // tile,),
        in_specs=[
            pl.BlockSpec((tile, width), lambda i: (i, 0)),
            pl.BlockSpec((group, width), lambda i: (0, 0)),
            pl.BlockSpec((tile, width), lambda i: (i, 0)),
        ],
        out_specs=[
            pl.BlockSpec((tile, width), lambda i: (i, 0)),
            pl.BlockSpec((tile, 128), lambda i: (i, 0)),
        ],
        out_shape=[
            jax.ShapeDtypeStruct((rows, width), jnp.float32),
            jax.ShapeDtypeStruct((rows, 128), jnp.float32),
        ],
        compiler_params=pltpu.CompilerParams(vmem_limit_bytes=48 * 1024 * 1024),
    )(queries, group_items, item_vectors)


def stats_block(q_ref, items_ref, stats_ref, *, scaling):
    scores = scaling * lax.dot_general(
        items_ref[...], q_ref[...], (((1,), (1,)), ((), ())), preferred_element_type=jnp.float32
    )
    highest = jnp.max(scores, axis=0, keepdims=True)
    stats_ref[0:1, :] = highest
    stats_ref[1:2, :] = jnp.sum(jnp.exp(scores - highest), axis=0, keepdims=True)


def block_stats(queries, items, scaling, tile=1024):
    rows, width = queries.shape
    tile = tile if rows % tile == 0 else rows
    return pl.pallas_call(
        functools.partial(stats_block, scaling=scaling),
        grid=(rows // tile,),
        in_specs=[pl.BlockSpec((tile, width), lambda i: (i, 0)), pl.BlockSpec(items.shape, lambda i: (0, 0))],
        out_specs=pl.BlockSpec((2, tile), lambda i: (0, i)),
        out_shape=jax.ShapeDtypeStruct((2, rows), jnp.float32),
        compiler_params=pltpu.CompilerParams(vmem_limit_bytes=48 * 1024 * 1024),
    )(queries, items)


def grads_block(q_ref, items_ref, totals_ref, pulled_ref, pushed_ref, *, scaling):
    scores = scaling * lax.dot_general(
        items_ref[...], q_ref[...], (((1,), (1,)), ((), ())), preferred_element_type=jnp.float32
    )
    soft = jnp.exp(scores - totals_ref[...]).astype(jnp.bfloat16)
    pulled_ref[...] = lax.dot_general(
        soft, items_ref[...], (((0,), (0,)), ((), ())), preferred_element_type=jnp.float32
    )
    part = jnp.dot(soft, q_ref[...], preferred_element_type=jnp.float32)

    @pl.when(pl.program_id(0) == 0)
    def _():
        pushed_ref[...] = part

    @pl.when(pl.program_id(0) != 0)
    def _():
        pushed_ref[...] += part


def block_grads_k(queries, items, totals, scaling, tile=1024):
    rows, width = queries.shape
    tile = tile if rows % tile == 0 else rows
    return pl.pallas_call(
        functools.partial(grads_block, scaling=scaling),
        grid=(rows // tile,),
        in_specs=[
            pl.BlockSpec((tile, width), lambda i: (i, 0)),
            pl.BlockSpec(items.shape, lambda i: (0, 0)),
            pl.BlockSpec((1, tile), lambda i: (0, i)),
        ],
        out_specs=[
            pl.BlockSpec((tile, width), lambda i: (i, 0)),
            pl.BlockSpec((items.shape[0], width), lambda i: (0, 0)),
        ],
        out_shape=[
            jax.ShapeDtypeStruct((rows, width), jnp.float32),
            jax.ShapeDtypeStruct((items.shape[0], width), jnp.float32),
        ],
        compiler_params=pltpu.CompilerParams(
            vmem_limit_bytes=48 * 1024 * 1024, dimension_semantics=("arbitrary",)
        ),
    )(queries, items, totals)


def plane_gather(value, axis, side):
    size = side * side
    index = lax.axis_index(axis)
    column = index % side
    line = index // side

    def shift(piece, step, along_row):
        pairs = []
        for source in range(size):
            high, low = divmod(source, side)
            if along_row:
                target = high * side + (low + step) % side
            else:
                target = ((high + step) % side) * side + low
            pairs.append((source, target))
        return lax.ppermute(piece, axis, pairs)

    pieces = jnp.stack([value] + [shift(value, step, True) for step in range(1, side)])
    row = jnp.concatenate([jnp.take(pieces, (column - c) % side, axis=0) for c in range(side)], axis=1)
    rows = jnp.stack([row] + [shift(row, step, False) for step in range(1, side)])
    return jnp.concatenate([jnp.take(rows, (line - r) % side, axis=0) for r in range(side)], axis=1)


def slot_index(live_slots, positions, slot_cap):
    ending = jnp.cumsum(live_slots)
    holder = jnp.sum((ending[None, :] <= positions[:, None]).astype(jnp.int32), axis=1)
    opening = ending - live_slots
    return holder * slot_cap + positions - jnp.take(opening, holder)


def tree_sum(value, axes, inner):
    total = 1
    for axis in axes:
        total *= lax.axis_size(axis)
    index = 0
    for axis in axes:
        index = index * lax.axis_size(axis) + lax.axis_index(axis)
    step = 1
    while step < inner and step < total and value.shape[0] % 2 == 0:
        half = value.shape[0] // 2
        upper = (index & step) != 0
        keep = jnp.where(upper, value[half:], value[:half])
        send = jnp.where(upper, value[:half], value[half:])
        value = keep + lax.ppermute(send, axes, [(i, i ^ step) for i in range(total)])
        step *= 2
    halved = step
    while step < total:
        value = value + lax.ppermute(value, axes, [(i, i ^ step) for i in range(total)])
        step *= 2
    step = halved // 2
    while step >= 1:
        got = lax.ppermute(value, axes, [(i, i ^ step) for i in range(total)])
        upper = (index & step) != 0
        value = jnp.where(upper, jnp.concatenate([got, value]), jnp.concatenate([value, got]))
        step //= 2
    return value


def butterfly_sum(value, axes):
    total = 1
    for axis in axes:
        total *= lax.axis_size(axis)
    step = 1
    while step < total:
        pairs = [(i, i ^ step) for i in range(total)]
        value = value + lax.ppermute(value, axes, pairs)
        step *= 2
    return value


def plane_shift(value, axis, side, step, along_row):
    pairs = []
    for source in range(side * side):
        high, low = divmod(source, side)
        if along_row:
            target = high * side + (low + step) % side
        else:
            target = ((high + step) % side) * side + low
        pairs.append((source, target))
    return lax.ppermute(value, axis, pairs)


def plane_gather_rows(value, axis, side, along_row):
    pieces = [value] + [plane_shift(value, axis, side, step, along_row) for step in range(1, side)]
    return jnp.concatenate(pieces, axis=0)


def plane_reduce_rows(value, axis, side, along_row):
    block = value.shape[0] // side
    total = value[:block]
    for step in range(1, side):
        part = value[((side - step) % side) * block:((side - step) % side + 1) * block]
        total = total + plane_shift(part, axis, side, step, along_row)
    return total


def block_grads(hidden, query_weight, item_vectors, axis, side, scaling):
    row_hidden = plane_gather_rows(hidden, axis, side, True)
    column_items = plane_gather_rows(item_vectors, axis, side, False)
    row_queries = jnp.dot(row_hidden, query_weight, preferred_element_type=jnp.float32).astype(jnp.bfloat16)
    stats = block_stats(row_queries, column_items, scaling)
    block = hidden.shape[0]
    gathered = [stats] + [
        jnp.roll(plane_shift(stats, axis, side, step, True), step * block, axis=1) for step in range(1, side)
    ]
    highest = gathered[0][0]
    for other in gathered[1:]:
        highest = jnp.maximum(highest, other[0])
    mass = gathered[0][1] * jnp.exp(gathered[0][0] - highest)
    for other in gathered[1:]:
        mass = mass + other[1] * jnp.exp(other[0] - highest)
    totals = highest + jnp.log(mass)
    pulled, pushed = block_grads_k(row_queries, column_items, totals.reshape(1, -1), scaling)
    weight_part = lax.dot_general(
        row_hidden, pulled, (((0,), (0,)), ((), ())),
        preferred_element_type=jnp.float32, precision=lax.Precision.HIGHEST,
    ) - lax.dot_general(
        hidden, item_vectors, (((0,), (0,)), ((), ())), preferred_element_type=jnp.float32
    )
    pushed = plane_reduce_rows(pushed, axis, side, False)
    item_grad = scaling * (pushed - row_queries[:block].astype(jnp.float32))
    return item_grad, scaling * weight_part


def local(item_table, query_table, query_weight, query_ids, fetch_rows, counts, example_pos):
    table_rows, model_width = item_table.shape
    sources = fetch_rows.shape[1]
    slot_cap = fetch_rows.shape[2]
    scaling = model_width ** (-0.5)
    requests = fetch_rows.reshape(sources, slot_cap)
    wanted = lax.all_to_all(requests, ("batch", "table"), split_axis=0, concat_axis=0, tiled=True)
    found_rows = jnp.take(item_table, wanted, axis=0)
    found_rows, query_ids = lax.optimization_barrier((found_rows, query_ids))
    fetched = lax.all_to_all(
        found_rows, ("batch", "table"), split_axis=0, concat_axis=0, tiled=True
    )
    slot_ids = slot_index(counts.reshape(sources), example_pos, slot_cap)
    item_vectors = jnp.take(fetched.reshape(sources * slot_cap, model_width), slot_ids, axis=0)
    looked = jnp.take(query_table, query_ids, axis=0).astype(jnp.float32)
    hidden = jnp.mean(looked, axis=1).astype(jnp.bfloat16)
    queries = jnp.dot(hidden, query_weight, preferred_element_type=jnp.float32).astype(jnp.bfloat16)
    side = int(round(lax.axis_size("batch") ** 0.5))
    if side * side == lax.axis_size("batch") and side > 1:
        item_grad, partial_value = block_grads(hidden, query_weight, item_vectors, "batch", side, scaling)
    else:
        group_queries = lax.all_gather(queries, "batch", axis=0, tiled=True)
        group_items = lax.all_gather(item_vectors, "batch", axis=0, tiled=True)
        query_grad, totals = forward(queries, group_items, item_vectors)
        side = int(round(lax.axis_size("batch") ** 0.5))
        if side * side == lax.axis_size("batch"):
            group_totals = plane_gather(totals[:, :1].reshape(1, -1), "batch", side)
        else:
            group_totals = lax.all_gather(totals[:, :1].reshape(1, -1), "batch", axis=1, tiled=True)
        scores_back = scaling * lax.dot_general(
            item_vectors, group_queries, (((1,), (1,)), ((), ())), preferred_element_type=jnp.float32
        )
        soft_back = jnp.exp(scores_back - group_totals).astype(jnp.bfloat16)
        summed = jnp.dot(soft_back, group_queries, preferred_element_type=jnp.float32)
        item_grad = scaling * (summed - queries.astype(jnp.float32))
        partial_value = lax.dot_general(
            hidden,
            query_grad.astype(jnp.bfloat16),
            (((0,), (0,)), ((), ())),
            preferred_element_type=jnp.float32,
        )
    total = lax.axis_size("batch") * lax.axis_size("table")
    if total & (total - 1) == 0:
        weight_grad = tree_sum(partial_value, ("batch", "table"), min(8, lax.axis_size("table")))
    else:
        weight_grad = lax.psum(partial_value, ("batch", "table"))
    item_grad, weight_grad = lax.optimization_barrier((item_grad, weight_grad))
    slot_grads = jax.ops.segment_sum(item_grad, slot_ids, num_segments=sources * slot_cap)
    slot_grads = slot_grads.reshape(sources, slot_cap, model_width)
    returned = lax.all_to_all(
        slot_grads, ("batch", "table"), split_axis=0, concat_axis=0, tiled=True
    )
    table_grad = (
        jnp.zeros((table_rows, model_width), jnp.float32)
        .at[wanted.reshape(-1)]
        .add(returned.reshape(-1, model_width))
    )
    return (table_grad, weight_grad)


def solution(mesh):
    in_specs = (
        P(("batch", "table"), None),
        P(),
        P(),
        P(("batch", "table"), None),
        P(("batch", "table"), None, None),
        P(("batch", "table"), None),
        P(("batch", "table")),
    )
    out_specs = (P(("batch", "table"), None), P())
    return jax.shard_map(local, mesh=mesh, in_specs=in_specs, out_specs=out_specs, check_vma=False)
```

```python
import functools

import jax
import jax.numpy as jnp
from jax import lax
from jax.experimental import pallas as pl
from jax.experimental.pallas import tpu as pltpu
from jax.sharding import PartitionSpec as P


def forward_block(q_ref, items_ref, own_ref, grad_ref, totals_ref, *, scaling):
    scores = scaling * lax.dot_general(
        q_ref[...], items_ref[...], (((1,), (1,)), ((), ())), preferred_element_type=jnp.float32
    )
    highest = jnp.max(scores, axis=1, keepdims=True)
    totals = highest + jnp.log(jnp.sum(jnp.exp(scores - highest), axis=1, keepdims=True))
    soft_weights = jnp.exp(scores - totals).astype(jnp.bfloat16)
    pulled = jnp.dot(soft_weights, items_ref[...], preferred_element_type=jnp.float32)
    grad_ref[...] = scaling * (pulled - own_ref[...].astype(jnp.float32))
    totals_ref[...] = jnp.broadcast_to(totals, totals_ref.shape)


def forward(queries, group_items, item_vectors, tile=256):
    rows, width = queries.shape
    group = group_items.shape[0]
    return pl.pallas_call(
        functools.partial(forward_block, scaling=width ** (-0.5)),
        grid=(rows // tile,),
        in_specs=[
            pl.BlockSpec((tile, width), lambda i: (i, 0)),
            pl.BlockSpec((group, width), lambda i: (0, 0)),
            pl.BlockSpec((tile, width), lambda i: (i, 0)),
        ],
        out_specs=[
            pl.BlockSpec((tile, width), lambda i: (i, 0)),
            pl.BlockSpec((tile, 128), lambda i: (i, 0)),
        ],
        out_shape=[
            jax.ShapeDtypeStruct((rows, width), jnp.float32),
            jax.ShapeDtypeStruct((rows, 128), jnp.float32),
        ],
        compiler_params=pltpu.CompilerParams(vmem_limit_bytes=48 * 1024 * 1024),
    )(queries, group_items, item_vectors)


def stats_block(q_ref, items_ref, stats_ref, *, scaling):
    scores = scaling * lax.dot_general(
        items_ref[...], q_ref[...], (((1,), (1,)), ((), ())), preferred_element_type=jnp.float32
    )
    highest = jnp.max(scores, axis=0, keepdims=True)
    stats_ref[0:1, :] = highest
    stats_ref[1:2, :] = jnp.sum(jnp.exp(scores - highest), axis=0, keepdims=True)


def block_stats(queries, items, scaling, tile=1024):
    rows, width = queries.shape
    tile = tile if rows % tile == 0 else rows
    return pl.pallas_call(
        functools.partial(stats_block, scaling=scaling),
        grid=(rows // tile,),
        in_specs=[pl.BlockSpec((tile, width), lambda i: (i, 0)), pl.BlockSpec(items.shape, lambda i: (0, 0))],
        out_specs=pl.BlockSpec((2, tile), lambda i: (0, i)),
        out_shape=jax.ShapeDtypeStruct((2, rows), jnp.float32),
        compiler_params=pltpu.CompilerParams(vmem_limit_bytes=48 * 1024 * 1024),
    )(queries, items)


def grads_block(q_ref, items_ref, totals_ref, pulled_ref, pushed_ref, *, scaling):
    scores = scaling * lax.dot_general(
        items_ref[...], q_ref[...], (((1,), (1,)), ((), ())), preferred_element_type=jnp.float32
    )
    soft = jnp.exp(scores - totals_ref[...]).astype(jnp.bfloat16)
    pulled_ref[...] = lax.dot_general(
        soft, items_ref[...], (((0,), (0,)), ((), ())), preferred_element_type=jnp.float32
    )
    part = jnp.dot(soft, q_ref[...], preferred_element_type=jnp.float32)

    @pl.when(pl.program_id(0) == 0)
    def _():
        pushed_ref[...] = part

    @pl.when(pl.program_id(0) != 0)
    def _():
        pushed_ref[...] += part


def block_grads_k(queries, items, totals, scaling, tile=1024):
    rows, width = queries.shape
    tile = tile if rows % tile == 0 else rows
    return pl.pallas_call(
        functools.partial(grads_block, scaling=scaling),
        grid=(rows // tile,),
        in_specs=[
            pl.BlockSpec((tile, width), lambda i: (i, 0)),
            pl.BlockSpec(items.shape, lambda i: (0, 0)),
            pl.BlockSpec((1, tile), lambda i: (0, i)),
        ],
        out_specs=[
            pl.BlockSpec((tile, width), lambda i: (i, 0)),
            pl.BlockSpec((items.shape[0], width), lambda i: (0, 0)),
        ],
        out_shape=[
            jax.ShapeDtypeStruct((rows, width), jnp.float32),
            jax.ShapeDtypeStruct((items.shape[0], width), jnp.float32),
        ],
        compiler_params=pltpu.CompilerParams(
            vmem_limit_bytes=48 * 1024 * 1024, dimension_semantics=("arbitrary",)
        ),
    )(queries, items, totals)


def plane_gather(value, axis, side):
    size = side * side
    index = lax.axis_index(axis)
    column = index % side
    line = index // side

    def shift(piece, step, along_row):
        pairs = []
        for source in range(size):
            high, low = divmod(source, side)
            if along_row:
                target = high * side + (low + step) % side
            else:
                target = ((high + step) % side) * side + low
            pairs.append((source, target))
        return lax.ppermute(piece, axis, pairs)

    pieces = jnp.stack([value] + [shift(value, step, True) for step in range(1, side)])
    row = jnp.concatenate([jnp.take(pieces, (column - c) % side, axis=0) for c in range(side)], axis=1)
    rows = jnp.stack([row] + [shift(row, step, False) for step in range(1, side)])
    return jnp.concatenate([jnp.take(rows, (line - r) % side, axis=0) for r in range(side)], axis=1)


def slot_index(live_slots, positions, slot_cap):
    ending = jnp.cumsum(live_slots)
    holder = jnp.sum((ending[None, :] <= positions[:, None]).astype(jnp.int32), axis=1)
    opening = ending - live_slots
    return holder * slot_cap + positions - jnp.take(opening, holder)


def tree_sum(value, axes, inner):
    total = 1
    for axis in axes:
        total *= lax.axis_size(axis)
    index = 0
    for axis in axes:
        index = index * lax.axis_size(axis) + lax.axis_index(axis)
    step = 1
    while step < inner and step < total and value.shape[0] % 2 == 0:
        half = value.shape[0] // 2
        upper = (index & step) != 0
        keep = jnp.where(upper, value[half:], value[:half])
        send = jnp.where(upper, value[:half], value[half:])
        value = keep + lax.ppermute(send, axes, [(i, i ^ step) for i in range(total)])
        step *= 2
    halved = step
    while step < total:
        value = value + lax.ppermute(value, axes, [(i, i ^ step) for i in range(total)])
        step *= 2
    step = halved // 2
    while step >= 1:
        got = lax.ppermute(value, axes, [(i, i ^ step) for i in range(total)])
        upper = (index & step) != 0
        value = jnp.where(upper, jnp.concatenate([got, value]), jnp.concatenate([value, got]))
        step //= 2
    return value


def plane_shift(value, axis, side, step, along_row):
    pairs = []
    for source in range(side * side):
        high, low = divmod(source, side)
        if along_row:
            target = high * side + (low + step) % side
        else:
            target = ((high + step) % side) * side + low
        pairs.append((source, target))
    return lax.ppermute(value, axis, pairs)


def plane_gather_rows(value, axis, side, along_row):
    pieces = [value] + [plane_shift(value, axis, side, step, along_row) for step in range(1, side)]
    return jnp.concatenate(pieces, axis=0)


def plane_reduce_rows(value, axis, side, along_row):
    block = value.shape[0] // side
    total = value[:block]
    for step in range(1, side):
        part = value[((side - step) % side) * block:((side - step) % side + 1) * block]
        total = total + plane_shift(part, axis, side, step, along_row)
    return total


def block_grads(hidden, query_weight, item_vectors, axis, side, scaling):
    row_hidden = plane_gather_rows(hidden, axis, side, True)
    column_items = plane_gather_rows(item_vectors, axis, side, False)
    row_queries = jnp.dot(row_hidden, query_weight, preferred_element_type=jnp.float32).astype(jnp.bfloat16)
    stats = block_stats(row_queries, column_items, scaling)
    block = hidden.shape[0]
    gathered = [stats] + [
        jnp.roll(plane_shift(stats, axis, side, step, True), step * block, axis=1) for step in range(1, side)
    ]
    highest = gathered[0][0]
    for other in gathered[1:]:
        highest = jnp.maximum(highest, other[0])
    mass = gathered[0][1] * jnp.exp(gathered[0][0] - highest)
    for other in gathered[1:]:
        mass = mass + other[1] * jnp.exp(other[0] - highest)
    totals = highest + jnp.log(mass)
    pulled, pushed = block_grads_k(row_queries, column_items, totals.reshape(1, -1), scaling)
    weight_part = lax.dot_general(
        row_hidden, pulled, (((0,), (0,)), ((), ())),
        preferred_element_type=jnp.float32, precision=lax.Precision.HIGHEST,
    ) - lax.dot_general(
        hidden, item_vectors, (((0,), (0,)), ((), ())), preferred_element_type=jnp.float32
    )
    pushed = plane_reduce_rows(pushed, axis, side, False)
    item_grad = scaling * (pushed - row_queries[:block].astype(jnp.float32))
    return item_grad, scaling * weight_part


def step_body(item_table, query_table, query_weight, query_ids, fetch_rows, counts, example_pos):
    table_rows, model_width = item_table.shape
    sources = fetch_rows.shape[1]
    slot_cap = fetch_rows.shape[2]
    scaling = model_width ** (-0.5)
    requests = fetch_rows.reshape(sources, slot_cap)
    wanted = lax.all_to_all(requests, ("batch", "table"), split_axis=0, concat_axis=0, tiled=True)
    found_rows = jnp.take(item_table, wanted, axis=0)
    found_rows, query_ids = lax.optimization_barrier((found_rows, query_ids))
    fetched = lax.all_to_all(
        found_rows, ("batch", "table"), split_axis=0, concat_axis=0, tiled=True
    )
    slot_ids = slot_index(counts.reshape(sources), example_pos, slot_cap)
    item_vectors = jnp.take(fetched.reshape(sources * slot_cap, model_width), slot_ids, axis=0)
    looked = jnp.take(query_table, query_ids, axis=0).astype(jnp.float32)
    hidden = jnp.mean(looked, axis=1).astype(jnp.bfloat16)
    queries = jnp.dot(hidden, query_weight, preferred_element_type=jnp.float32).astype(jnp.bfloat16)
    side = int(round(lax.axis_size("batch") ** 0.5))
    if side * side == lax.axis_size("batch") and side > 1:
        item_grad, partial_value = block_grads(hidden, query_weight, item_vectors, "batch", side, scaling)
    else:
        group_queries = lax.all_gather(queries, "batch", axis=0, tiled=True)
        group_items = lax.all_gather(item_vectors, "batch", axis=0, tiled=True)
        query_grad, totals = forward(queries, group_items, item_vectors)
        side = int(round(lax.axis_size("batch") ** 0.5))
        if side * side == lax.axis_size("batch"):
            group_totals = plane_gather(totals[:, :1].reshape(1, -1), "batch", side)
        else:
            group_totals = lax.all_gather(totals[:, :1].reshape(1, -1), "batch", axis=1, tiled=True)
        scores_back = scaling * lax.dot_general(
            item_vectors, group_queries, (((1,), (1,)), ((), ())), preferred_element_type=jnp.float32
        )
        soft_back = jnp.exp(scores_back - group_totals).astype(jnp.bfloat16)
        summed = jnp.dot(soft_back, group_queries, preferred_element_type=jnp.float32)
        item_grad = scaling * (summed - queries.astype(jnp.float32))
        partial_value = lax.dot_general(
            hidden,
            query_grad.astype(jnp.bfloat16),
            (((0,), (0,)), ((), ())),
            preferred_element_type=jnp.float32,
        )
    total = lax.axis_size("batch") * lax.axis_size("table")
    if total & (total - 1) == 0:
        weight_grad = tree_sum(partial_value, ("batch", "table"), min(8, lax.axis_size("table")))
    else:
        weight_grad = lax.psum(partial_value, ("batch", "table"))
    item_grad, weight_grad = lax.optimization_barrier((item_grad, weight_grad))
    slot_grads = jax.ops.segment_sum(item_grad, slot_ids, num_segments=sources * slot_cap)
    slot_grads = slot_grads.reshape(sources, slot_cap, model_width)
    returned = lax.all_to_all(
        slot_grads, ("batch", "table"), split_axis=0, concat_axis=0, tiled=True
    )
    table_grad = (
        jnp.zeros((table_rows, model_width), jnp.float32)
        .at[wanted.reshape(-1)]
        .add(returned.reshape(-1, model_width))
    )
    return (table_grad, weight_grad)


def solution(mesh):
    in_specs = (
        P(("batch", "table"), None),
        P(),
        P(),
        P(("batch", "table"), None),
        P(("batch", "table"), None, None),
        P(("batch", "table"), None),
        P(("batch", "table")),
    )
    out_specs = (P(("batch", "table"), None), P())
    return jax.shard_map(step_body, mesh=mesh, in_specs=in_specs, out_specs=out_specs, check_vma=False)
```

```python
import functools

import jax
import jax.numpy as jnp
from jax import lax
from jax.experimental import pallas as pl
from jax.experimental.pallas import tpu as pltpu
from jax.sharding import PartitionSpec as P


def forward_block(q_ref, items_ref, own_ref, grad_ref, totals_ref, *, scaling):
    scores = scaling * lax.dot_general(
        q_ref[...], items_ref[...], (((1,), (1,)), ((), ())), preferred_element_type=jnp.float32
    )
    highest = jnp.max(scores, axis=1, keepdims=True)
    totals = highest + jnp.log(jnp.sum(jnp.exp(scores - highest), axis=1, keepdims=True))
    soft_weights = jnp.exp(scores - totals).astype(jnp.bfloat16)
    pulled = jnp.dot(soft_weights, items_ref[...], preferred_element_type=jnp.float32)
    grad_ref[...] = scaling * (pulled - own_ref[...].astype(jnp.float32))
    totals_ref[...] = jnp.broadcast_to(totals, totals_ref.shape)


def forward(queries, group_items, item_vectors, tile=256):
    rows, width = queries.shape
    group = group_items.shape[0]
    return pl.pallas_call(
        functools.partial(forward_block, scaling=width ** (-0.5)),
        grid=(rows // tile,),
        in_specs=[
            pl.BlockSpec((tile, width), lambda i: (i, 0)),
            pl.BlockSpec((group, width), lambda i: (0, 0)),
            pl.BlockSpec((tile, width), lambda i: (i, 0)),
        ],
        out_specs=[
            pl.BlockSpec((tile, width), lambda i: (i, 0)),
            pl.BlockSpec((tile, 128), lambda i: (i, 0)),
        ],
        out_shape=[
            jax.ShapeDtypeStruct((rows, width), jnp.float32),
            jax.ShapeDtypeStruct((rows, 128), jnp.float32),
        ],
        compiler_params=pltpu.CompilerParams(vmem_limit_bytes=48 * 1024 * 1024),
    )(queries, group_items, item_vectors)


def stats_block(q_ref, items_ref, stats_ref, *, scaling):
    scores = scaling * lax.dot_general(
        items_ref[...], q_ref[...], (((1,), (1,)), ((), ())), preferred_element_type=jnp.float32
    )
    highest = jnp.max(scores, axis=0, keepdims=True)
    stats_ref[0:1, :] = highest
    stats_ref[1:2, :] = jnp.sum(jnp.exp(scores - highest), axis=0, keepdims=True)


def block_stats(queries, items, scaling, tile=1024):
    rows, width = queries.shape
    tile = tile if rows % tile == 0 else rows
    return pl.pallas_call(
        functools.partial(stats_block, scaling=scaling),
        grid=(rows // tile,),
        in_specs=[pl.BlockSpec((tile, width), lambda i: (i, 0)), pl.BlockSpec(items.shape, lambda i: (0, 0))],
        out_specs=pl.BlockSpec((2, tile), lambda i: (0, i)),
        out_shape=jax.ShapeDtypeStruct((2, rows), jnp.float32),
        compiler_params=pltpu.CompilerParams(vmem_limit_bytes=48 * 1024 * 1024),
    )(queries, items)


def grads_block(q_ref, items_ref, totals_ref, pulled_ref, pushed_ref, *, scaling):
    scores = scaling * lax.dot_general(
        items_ref[...], q_ref[...], (((1,), (1,)), ((), ())), preferred_element_type=jnp.float32
    )
    soft = jnp.exp(scores - totals_ref[...]).astype(jnp.bfloat16)
    pulled_ref[...] = lax.dot_general(
        soft, items_ref[...], (((0,), (0,)), ((), ())), preferred_element_type=jnp.float32
    )
    part = jnp.dot(soft, q_ref[...], preferred_element_type=jnp.float32)

    @pl.when(pl.program_id(0) == 0)
    def _():
        pushed_ref[...] = part

    @pl.when(pl.program_id(0) != 0)
    def _():
        pushed_ref[...] += part


def block_grads_k(queries, items, totals, scaling, tile=1024):
    rows, width = queries.shape
    tile = tile if rows % tile == 0 else rows
    return pl.pallas_call(
        functools.partial(grads_block, scaling=scaling),
        grid=(rows // tile,),
        in_specs=[
            pl.BlockSpec((tile, width), lambda i: (i, 0)),
            pl.BlockSpec(items.shape, lambda i: (0, 0)),
            pl.BlockSpec((1, tile), lambda i: (0, i)),
        ],
        out_specs=[
            pl.BlockSpec((tile, width), lambda i: (i, 0)),
            pl.BlockSpec((items.shape[0], width), lambda i: (0, 0)),
        ],
        out_shape=[
            jax.ShapeDtypeStruct((rows, width), jnp.float32),
            jax.ShapeDtypeStruct((items.shape[0], width), jnp.float32),
        ],
        compiler_params=pltpu.CompilerParams(
            vmem_limit_bytes=48 * 1024 * 1024, dimension_semantics=("arbitrary",)
        ),
    )(queries, items, totals)


def plane_gather(value, axis, side):
    size = side * side
    index = lax.axis_index(axis)
    column = index % side
    line = index // side

    def shift(piece, step, along_row):
        pairs = []
        for source in range(size):
            high, low = divmod(source, side)
            if along_row:
                target = high * side + (low + step) % side
            else:
                target = ((high + step) % side) * side + low
            pairs.append((source, target))
        return lax.ppermute(piece, axis, pairs)

    pieces = jnp.stack([value] + [shift(value, step, True) for step in range(1, side)])
    row = jnp.concatenate([jnp.take(pieces, (column - c) % side, axis=0) for c in range(side)], axis=1)
    rows = jnp.stack([row] + [shift(row, step, False) for step in range(1, side)])
    return jnp.concatenate([jnp.take(rows, (line - r) % side, axis=0) for r in range(side)], axis=1)


def slot_index(live_slots, positions, slot_cap):
    ending = jnp.cumsum(live_slots)
    holder = jnp.sum((ending[None, :] <= positions[:, None]).astype(jnp.int32), axis=1)
    opening = ending - live_slots
    return holder * slot_cap + positions - jnp.take(opening, holder)


def tree_sum(value, axes, inner):
    total = 1
    for axis in axes:
        total *= lax.axis_size(axis)
    index = 0
    for axis in axes:
        index = index * lax.axis_size(axis) + lax.axis_index(axis)
    step = 1
    while step < inner and step < total and value.shape[0] % 2 == 0:
        half = value.shape[0] // 2
        upper = (index & step) != 0
        keep = jnp.where(upper, value[half:], value[:half])
        send = jnp.where(upper, value[:half], value[half:])
        value = keep + lax.ppermute(send, axes, [(i, i ^ step) for i in range(total)])
        step *= 2
    halved = step
    while step < total:
        value = value + lax.ppermute(value, axes, [(i, i ^ step) for i in range(total)])
        step *= 2
    step = halved // 2
    while step >= 1:
        got = lax.ppermute(value, axes, [(i, i ^ step) for i in range(total)])
        upper = (index & step) != 0
        value = jnp.where(upper, jnp.concatenate([got, value]), jnp.concatenate([value, got]))
        step //= 2
    return value


def plane_shift(value, axis, side, step, along_row):
    pairs = []
    for source in range(side * side):
        high, low = divmod(source, side)
        if along_row:
            target = high * side + (low + step) % side
        else:
            target = ((high + step) % side) * side + low
        pairs.append((source, target))
    return lax.ppermute(value, axis, pairs)


def plane_gather_rows(value, axis, side, along_row):
    pieces = [value] + [plane_shift(value, axis, side, step, along_row) for step in range(1, side)]
    return jnp.concatenate(pieces, axis=0)


def plane_reduce_rows(value, axis, side, along_row):
    block = value.shape[0] // side
    total = value[:block]
    for step in range(1, side):
        part = value[((side - step) % side) * block:((side - step) % side + 1) * block]
        total = total + plane_shift(part, axis, side, step, along_row)
    return total


def block_grads(hidden, query_weight, item_vectors, axis, side, scaling):
    row_hidden = plane_gather_rows(hidden, axis, side, True)
    column_items = plane_gather_rows(item_vectors, axis, side, False)
    row_queries = jnp.dot(row_hidden, query_weight, preferred_element_type=jnp.float32).astype(jnp.bfloat16)
    stats = block_stats(row_queries, column_items, scaling)
    block = hidden.shape[0]
    gathered = [stats] + [
        jnp.roll(plane_shift(stats, axis, side, step, True), step * block, axis=1) for step in range(1, side)
    ]
    highest = gathered[0][0]
    for other in gathered[1:]:
        highest = jnp.maximum(highest, other[0])
    mass = gathered[0][1] * jnp.exp(gathered[0][0] - highest)
    for other in gathered[1:]:
        mass = mass + other[1] * jnp.exp(other[0] - highest)
    totals = highest + jnp.log(mass)
    pulled, pushed = block_grads_k(row_queries, column_items, totals.reshape(1, -1), scaling)
    weight_part = lax.dot_general(
        row_hidden, pulled, (((0,), (0,)), ((), ())),
        preferred_element_type=jnp.float32, precision=lax.Precision.HIGHEST,
    ) - lax.dot_general(
        hidden, item_vectors, (((0,), (0,)), ((), ())), preferred_element_type=jnp.float32
    )
    pushed = plane_reduce_rows(pushed, axis, side, False)
    item_grad = scaling * (pushed - row_queries[:block].astype(jnp.float32))
    return item_grad, scaling * weight_part


def step_body(item_table, query_table, query_weight, query_ids, fetch_rows, counts, example_pos):
    table_rows, model_width = item_table.shape
    sources = fetch_rows.shape[1]
    slot_cap = fetch_rows.shape[2]
    scaling = model_width ** (-0.5)
    requests = fetch_rows.reshape(sources, slot_cap)
    wanted = lax.all_to_all(requests, ("batch", "table"), split_axis=0, concat_axis=0, tiled=True)
    found_rows = jnp.take(item_table, wanted, axis=0)
    found_rows, query_ids = lax.optimization_barrier((found_rows, query_ids))
    fetched = lax.all_to_all(
        found_rows, ("batch", "table"), split_axis=0, concat_axis=0, tiled=True
    )
    slot_ids = slot_index(counts.reshape(sources), example_pos, slot_cap)
    item_vectors = jnp.take(fetched.reshape(sources * slot_cap, model_width), slot_ids, axis=0)
    looked = jnp.take(query_table, query_ids, axis=0).astype(jnp.float32)
    hidden = jnp.mean(looked, axis=1).astype(jnp.bfloat16)
    queries = jnp.dot(hidden, query_weight, preferred_element_type=jnp.float32).astype(jnp.bfloat16)
    side = int(round(lax.axis_size("batch") ** 0.5))
    if side * side == lax.axis_size("batch") and side > 1:
        item_grad, partial_value = block_grads(hidden, query_weight, item_vectors, "batch", side, scaling)
    else:
        group_queries = lax.all_gather(queries, "batch", axis=0, tiled=True)
        group_items = lax.all_gather(item_vectors, "batch", axis=0, tiled=True)
        query_grad, totals = forward(queries, group_items, item_vectors)
        side = int(round(lax.axis_size("batch") ** 0.5))
        if side * side == lax.axis_size("batch"):
            group_totals = plane_gather(totals[:, :1].reshape(1, -1), "batch", side)
        else:
            group_totals = lax.all_gather(totals[:, :1].reshape(1, -1), "batch", axis=1, tiled=True)
        scores_back = scaling * lax.dot_general(
            item_vectors, group_queries, (((1,), (1,)), ((), ())), preferred_element_type=jnp.float32
        )
        soft_back = jnp.exp(scores_back - group_totals).astype(jnp.bfloat16)
        summed = jnp.dot(soft_back, group_queries, preferred_element_type=jnp.float32)
        item_grad = scaling * (summed - queries.astype(jnp.float32))
        partial_value = lax.dot_general(
            hidden,
            query_grad.astype(jnp.bfloat16),
            (((0,), (0,)), ((), ())),
            preferred_element_type=jnp.float32,
        )
    total = lax.axis_size("batch") * lax.axis_size("table")
    if total & (total - 1) == 0:
        weight_grad = tree_sum(partial_value, ("batch", "table"), min(8, lax.axis_size("table")))
    else:
        weight_grad = lax.psum(partial_value, ("batch", "table"))
    item_grad, weight_grad = lax.optimization_barrier((item_grad, weight_grad))
    chosen = (lax.broadcasted_iota(jnp.int32, (sources * slot_cap, slot_ids.shape[0]), 0) == slot_ids[None, :])
    slot_grads = jnp.dot(
        chosen.astype(jnp.bfloat16), item_grad,
        preferred_element_type=jnp.float32, precision=lax.Precision.HIGHEST,
    )
    slot_grads = slot_grads.reshape(sources, slot_cap, model_width)
    returned = lax.all_to_all(
        slot_grads, ("batch", "table"), split_axis=0, concat_axis=0, tiled=True
    )
    table_grad = (
        jnp.zeros((table_rows, model_width), jnp.float32)
        .at[wanted.reshape(-1)]
        .add(returned.reshape(-1, model_width))
    )
    return (table_grad, weight_grad)


def solution(mesh):
    in_specs = (
        P(("batch", "table"), None),
        P(),
        P(),
        P(("batch", "table"), None),
        P(("batch", "table"), None, None),
        P(("batch", "table"), None),
        P(("batch", "table")),
    )
    out_specs = (P(("batch", "table"), None), P())
    return jax.shard_map(step_body, mesh=mesh, in_specs=in_specs, out_specs=out_specs, check_vma=False)
```

```python
import functools

import jax
import jax.numpy as jnp
from jax import lax
from jax.experimental import pallas as pl
from jax.experimental.pallas import tpu as pltpu
from jax.sharding import PartitionSpec as P


def forward_block(q_ref, items_ref, own_ref, grad_ref, totals_ref, *, scaling):
    scores = scaling * lax.dot_general(
        q_ref[...], items_ref[...], (((1,), (1,)), ((), ())), preferred_element_type=jnp.float32
    )
    highest = jnp.max(scores, axis=1, keepdims=True)
    totals = highest + jnp.log(jnp.sum(jnp.exp(scores - highest), axis=1, keepdims=True))
    soft_weights = jnp.exp(scores - totals).astype(jnp.bfloat16)
    pulled = jnp.dot(soft_weights, items_ref[...], preferred_element_type=jnp.float32)
    grad_ref[...] = scaling * (pulled - own_ref[...].astype(jnp.float32))
    totals_ref[...] = jnp.broadcast_to(totals, totals_ref.shape)


def forward(queries, group_items, item_vectors, tile=256):
    rows, width = queries.shape
    group = group_items.shape[0]
    return pl.pallas_call(
        functools.partial(forward_block, scaling=width ** (-0.5)),
        grid=(rows // tile,),
        in_specs=[
            pl.BlockSpec((tile, width), lambda i: (i, 0)),
            pl.BlockSpec((group, width), lambda i: (0, 0)),
            pl.BlockSpec((tile, width), lambda i: (i, 0)),
        ],
        out_specs=[
            pl.BlockSpec((tile, width), lambda i: (i, 0)),
            pl.BlockSpec((tile, 128), lambda i: (i, 0)),
        ],
        out_shape=[
            jax.ShapeDtypeStruct((rows, width), jnp.float32),
            jax.ShapeDtypeStruct((rows, 128), jnp.float32),
        ],
        compiler_params=pltpu.CompilerParams(vmem_limit_bytes=48 * 1024 * 1024),
    )(queries, group_items, item_vectors)


def stats_block(q_ref, items_ref, stats_ref, *, scaling):
    scores = scaling * lax.dot_general(
        items_ref[...], q_ref[...], (((1,), (1,)), ((), ())), preferred_element_type=jnp.float32
    )
    highest = jnp.max(scores, axis=0, keepdims=True)
    stats_ref[0:1, :] = highest
    stats_ref[1:2, :] = jnp.sum(jnp.exp(scores - highest), axis=0, keepdims=True)


def block_stats(queries, items, scaling, tile=1024):
    rows, width = queries.shape
    tile = tile if rows % tile == 0 else rows
    return pl.pallas_call(
        functools.partial(stats_block, scaling=scaling),
        grid=(rows // tile,),
        in_specs=[pl.BlockSpec((tile, width), lambda i: (i, 0)), pl.BlockSpec(items.shape, lambda i: (0, 0))],
        out_specs=pl.BlockSpec((2, tile), lambda i: (0, i)),
        out_shape=jax.ShapeDtypeStruct((2, rows), jnp.float32),
        compiler_params=pltpu.CompilerParams(vmem_limit_bytes=48 * 1024 * 1024),
    )(queries, items)


def grads_block(q_ref, items_ref, totals_ref, pulled_ref, pushed_ref, *, scaling):
    scores = scaling * lax.dot_general(
        items_ref[...], q_ref[...], (((1,), (1,)), ((), ())), preferred_element_type=jnp.float32
    )
    soft = jnp.exp(scores - totals_ref[...]).astype(jnp.bfloat16)
    pulled_ref[...] = lax.dot_general(
        soft, items_ref[...], (((0,), (0,)), ((), ())), preferred_element_type=jnp.float32
    )
    part = jnp.dot(soft, q_ref[...], preferred_element_type=jnp.float32)

    @pl.when(pl.program_id(0) == 0)
    def _():
        pushed_ref[...] = part

    @pl.when(pl.program_id(0) != 0)
    def _():
        pushed_ref[...] += part


def block_grads_k(queries, items, totals, scaling, tile=1024):
    rows, width = queries.shape
    tile = tile if rows % tile == 0 else rows
    return pl.pallas_call(
        functools.partial(grads_block, scaling=scaling),
        grid=(rows // tile,),
        in_specs=[
            pl.BlockSpec((tile, width), lambda i: (i, 0)),
            pl.BlockSpec(items.shape, lambda i: (0, 0)),
            pl.BlockSpec((1, tile), lambda i: (0, i)),
        ],
        out_specs=[
            pl.BlockSpec((tile, width), lambda i: (i, 0)),
            pl.BlockSpec((items.shape[0], width), lambda i: (0, 0)),
        ],
        out_shape=[
            jax.ShapeDtypeStruct((rows, width), jnp.float32),
            jax.ShapeDtypeStruct((items.shape[0], width), jnp.float32),
        ],
        compiler_params=pltpu.CompilerParams(
            vmem_limit_bytes=48 * 1024 * 1024, dimension_semantics=("arbitrary",)
        ),
    )(queries, items, totals)


def plane_gather(value, axis, side):
    size = side * side
    index = lax.axis_index(axis)
    column = index % side
    line = index // side

    def shift(piece, step, along_row):
        pairs = []
        for source in range(size):
            high, low = divmod(source, side)
            if along_row:
                target = high * side + (low + step) % side
            else:
                target = ((high + step) % side) * side + low
            pairs.append((source, target))
        return lax.ppermute(piece, axis, pairs)

    pieces = jnp.stack([value] + [shift(value, step, True) for step in range(1, side)])
    row = jnp.concatenate([jnp.take(pieces, (column - c) % side, axis=0) for c in range(side)], axis=1)
    rows = jnp.stack([row] + [shift(row, step, False) for step in range(1, side)])
    return jnp.concatenate([jnp.take(rows, (line - r) % side, axis=0) for r in range(side)], axis=1)


def slot_index(live_slots, positions, slot_cap):
    ending = jnp.cumsum(live_slots)
    holder = jnp.sum((ending[None, :] <= positions[:, None]).astype(jnp.int32), axis=1)
    opening = ending - live_slots
    return holder * slot_cap + positions - jnp.take(opening, holder)


def tree_sum(value, axes, inner):
    total = 1
    for axis in axes:
        total *= lax.axis_size(axis)
    index = 0
    for axis in axes:
        index = index * lax.axis_size(axis) + lax.axis_index(axis)
    step = 1
    while step < inner and step < total and value.shape[0] % 2 == 0:
        half = value.shape[0] // 2
        upper = (index & step) != 0
        keep = jnp.where(upper, value[half:], value[:half])
        send = jnp.where(upper, value[:half], value[half:])
        value = keep + lax.ppermute(send, axes, [(i, i ^ step) for i in range(total)])
        step *= 2
    halved = step
    while step < total:
        value = value + lax.ppermute(value, axes, [(i, i ^ step) for i in range(total)])
        step *= 2
    step = halved // 2
    while step >= 1:
        got = lax.ppermute(value, axes, [(i, i ^ step) for i in range(total)])
        upper = (index & step) != 0
        value = jnp.where(upper, jnp.concatenate([got, value]), jnp.concatenate([value, got]))
        step //= 2
    return value


def plane_shift(value, axis, side, step, along_row):
    pairs = []
    for source in range(side * side):
        high, low = divmod(source, side)
        if along_row:
            target = high * side + (low + step) % side
        else:
            target = ((high + step) % side) * side + low
        pairs.append((source, target))
    return lax.ppermute(value, axis, pairs)


def plane_gather_rows(value, axis, side, along_row):
    pieces = [value] + [plane_shift(value, axis, side, step, along_row) for step in range(1, side)]
    return jnp.concatenate(pieces, axis=0)


def plane_reduce_rows(value, axis, side, along_row):
    block = value.shape[0] // side
    total = value[:block]
    for step in range(1, side):
        part = value[((side - step) % side) * block:((side - step) % side + 1) * block]
        total = total + plane_shift(part, axis, side, step, along_row)
    return total


def block_grads(hidden, query_weight, item_vectors, axis, side, scaling):
    row_hidden = plane_gather_rows(hidden, axis, side, True)
    column_items = plane_gather_rows(item_vectors, axis, side, False)
    row_queries = jnp.dot(row_hidden, query_weight, preferred_element_type=jnp.float32).astype(jnp.bfloat16)
    stats = block_stats(row_queries, column_items, scaling)
    block = hidden.shape[0]
    gathered = [stats] + [
        jnp.roll(plane_shift(stats, axis, side, step, True), step * block, axis=1) for step in range(1, side)
    ]
    highest = gathered[0][0]
    for other in gathered[1:]:
        highest = jnp.maximum(highest, other[0])
    mass = gathered[0][1] * jnp.exp(gathered[0][0] - highest)
    for other in gathered[1:]:
        mass = mass + other[1] * jnp.exp(other[0] - highest)
    totals = highest + jnp.log(mass)
    pulled, pushed = block_grads_k(row_queries, column_items, totals.reshape(1, -1), scaling)
    weight_part = lax.dot_general(
        row_hidden, pulled, (((0,), (0,)), ((), ())),
        preferred_element_type=jnp.float32, precision=lax.Precision.HIGHEST,
    ) - lax.dot_general(
        hidden, item_vectors, (((0,), (0,)), ((), ())), preferred_element_type=jnp.float32
    )
    pushed = plane_reduce_rows(pushed, axis, side, False)
    item_grad = scaling * (pushed - row_queries[:block].astype(jnp.float32))
    return item_grad, scaling * weight_part


def step_body(item_table, query_table, query_weight, query_ids, fetch_rows, counts, example_pos):
    table_rows, model_width = item_table.shape
    sources = fetch_rows.shape[1]
    slot_cap = fetch_rows.shape[2]
    scaling = model_width ** (-0.5)
    requests = fetch_rows.reshape(sources, slot_cap)
    wanted = lax.all_to_all(requests, ("batch", "table"), split_axis=0, concat_axis=0, tiled=True)
    found_rows = jnp.take(item_table, wanted, axis=0)
    found_rows, query_ids = lax.optimization_barrier((found_rows, query_ids))
    fetched = lax.all_to_all(
        found_rows, ("batch", "table"), split_axis=0, concat_axis=0, tiled=True
    )
    slot_ids = slot_index(counts.reshape(sources), example_pos, slot_cap)
    item_vectors = jnp.take(fetched.reshape(sources * slot_cap, model_width), slot_ids, axis=0)
    looked = jnp.take(query_table, query_ids, axis=0).astype(jnp.float32)
    hidden = jnp.mean(looked, axis=1).astype(jnp.bfloat16)
    queries = jnp.dot(hidden, query_weight, preferred_element_type=jnp.float32).astype(jnp.bfloat16)
    side = int(round(lax.axis_size("batch") ** 0.5))
    if side * side == lax.axis_size("batch") and side > 1:
        item_grad, partial_value = block_grads(hidden, query_weight, item_vectors, "batch", side, scaling)
    else:
        group_queries = lax.all_gather(queries, "batch", axis=0, tiled=True)
        group_items = lax.all_gather(item_vectors, "batch", axis=0, tiled=True)
        query_grad, totals = forward(queries, group_items, item_vectors)
        side = int(round(lax.axis_size("batch") ** 0.5))
        if side * side == lax.axis_size("batch"):
            group_totals = plane_gather(totals[:, :1].reshape(1, -1), "batch", side)
        else:
            group_totals = lax.all_gather(totals[:, :1].reshape(1, -1), "batch", axis=1, tiled=True)
        scores_back = scaling * lax.dot_general(
            item_vectors, group_queries, (((1,), (1,)), ((), ())), preferred_element_type=jnp.float32
        )
        soft_back = jnp.exp(scores_back - group_totals).astype(jnp.bfloat16)
        summed = jnp.dot(soft_back, group_queries, preferred_element_type=jnp.float32)
        item_grad = scaling * (summed - queries.astype(jnp.float32))
        partial_value = lax.dot_general(
            hidden,
            query_grad.astype(jnp.bfloat16),
            (((0,), (0,)), ((), ())),
            preferred_element_type=jnp.float32,
        )
    total = lax.axis_size("batch") * lax.axis_size("table")
    if total & (total - 1) == 0:
        weight_grad = tree_sum(partial_value, ("batch", "table"), min(4, lax.axis_size("table")))
    else:
        weight_grad = lax.psum(partial_value, ("batch", "table"))
    item_grad, weight_grad = lax.optimization_barrier((item_grad, weight_grad))
    chosen = (lax.broadcasted_iota(jnp.int32, (sources * slot_cap, slot_ids.shape[0]), 0) == slot_ids[None, :])
    slot_grads = jnp.dot(
        chosen.astype(jnp.bfloat16), item_grad,
        preferred_element_type=jnp.float32, precision=lax.Precision.HIGHEST,
    )
    slot_grads = slot_grads.reshape(sources, slot_cap, model_width)
    returned = lax.all_to_all(
        slot_grads, ("batch", "table"), split_axis=0, concat_axis=0, tiled=True
    )
    landing = (
        lax.broadcasted_iota(jnp.int32, (table_rows, wanted.size), 0) == wanted.reshape(1, -1)
    )
    table_grad = jnp.dot(
        landing.astype(jnp.bfloat16), returned.reshape(-1, model_width),
        preferred_element_type=jnp.float32, precision=lax.Precision.HIGHEST,
    )
    return (table_grad, weight_grad)


def solution(mesh):
    in_specs = (
        P(("batch", "table"), None),
        P(),
        P(),
        P(("batch", "table"), None),
        P(("batch", "table"), None, None),
        P(("batch", "table"), None),
        P(("batch", "table")),
    )
    out_specs = (P(("batch", "table"), None), P())
    return jax.shard_map(step_body, mesh=mesh, in_specs=in_specs, out_specs=out_specs, check_vma=False)
```

```python
import functools

import jax
import jax.numpy as jnp
from jax import lax
from jax.experimental import pallas as pl
from jax.experimental.pallas import tpu as pltpu
from jax.sharding import PartitionSpec as P


def forward_block(q_ref, items_ref, own_ref, grad_ref, totals_ref, *, scaling):
    scores = scaling * lax.dot_general(
        q_ref[...], items_ref[...], (((1,), (1,)), ((), ())), preferred_element_type=jnp.float32
    )
    highest = jnp.max(scores, axis=1, keepdims=True)
    totals = highest + jnp.log(jnp.sum(jnp.exp(scores - highest), axis=1, keepdims=True))
    soft_weights = jnp.exp(scores - totals).astype(jnp.bfloat16)
    pulled = jnp.dot(soft_weights, items_ref[...], preferred_element_type=jnp.float32)
    grad_ref[...] = scaling * (pulled - own_ref[...].astype(jnp.float32))
    totals_ref[...] = jnp.broadcast_to(totals, totals_ref.shape)


def forward(queries, group_items, item_vectors, tile=256):
    rows, width = queries.shape
    group = group_items.shape[0]
    return pl.pallas_call(
        functools.partial(forward_block, scaling=width ** (-0.5)),
        grid=(rows // tile,),
        in_specs=[
            pl.BlockSpec((tile, width), lambda i: (i, 0)),
            pl.BlockSpec((group, width), lambda i: (0, 0)),
            pl.BlockSpec((tile, width), lambda i: (i, 0)),
        ],
        out_specs=[
            pl.BlockSpec((tile, width), lambda i: (i, 0)),
            pl.BlockSpec((tile, 128), lambda i: (i, 0)),
        ],
        out_shape=[
            jax.ShapeDtypeStruct((rows, width), jnp.float32),
            jax.ShapeDtypeStruct((rows, 128), jnp.float32),
        ],
        compiler_params=pltpu.CompilerParams(vmem_limit_bytes=48 * 1024 * 1024),
    )(queries, group_items, item_vectors)


def stats_block(q_ref, items_ref, stats_ref, *, scaling):
    scores = scaling * lax.dot_general(
        items_ref[...], q_ref[...], (((1,), (1,)), ((), ())), preferred_element_type=jnp.float32
    )
    highest = jnp.max(scores, axis=0, keepdims=True)
    stats_ref[0:1, :] = highest
    stats_ref[1:2, :] = jnp.sum(jnp.exp(scores - highest), axis=0, keepdims=True)


def block_stats(queries, items, scaling, tile=2048):
    rows, width = queries.shape
    tile = tile if rows % tile == 0 else rows
    return pl.pallas_call(
        functools.partial(stats_block, scaling=scaling),
        grid=(rows // tile,),
        in_specs=[pl.BlockSpec((tile, width), lambda i: (i, 0)), pl.BlockSpec(items.shape, lambda i: (0, 0))],
        out_specs=pl.BlockSpec((2, tile), lambda i: (0, i)),
        out_shape=jax.ShapeDtypeStruct((2, rows), jnp.float32),
        compiler_params=pltpu.CompilerParams(vmem_limit_bytes=48 * 1024 * 1024),
    )(queries, items)


def grads_block(q_ref, items_ref, totals_ref, pulled_ref, pushed_ref, *, scaling):
    scores = scaling * lax.dot_general(
        items_ref[...], q_ref[...], (((1,), (1,)), ((), ())), preferred_element_type=jnp.float32
    )
    soft = jnp.exp(scores - totals_ref[...]).astype(jnp.bfloat16)
    pulled_ref[...] = lax.dot_general(
        soft, items_ref[...], (((0,), (0,)), ((), ())), preferred_element_type=jnp.float32
    )
    part = jnp.dot(soft, q_ref[...], preferred_element_type=jnp.float32)

    @pl.when(pl.program_id(0) == 0)
    def _():
        pushed_ref[...] = part

    @pl.when(pl.program_id(0) != 0)
    def _():
        pushed_ref[...] += part


def block_grads_k(queries, items, totals, scaling, tile=2048):
    rows, width = queries.shape
    tile = tile if rows % tile == 0 else rows
    return pl.pallas_call(
        functools.partial(grads_block, scaling=scaling),
        grid=(rows // tile,),
        in_specs=[
            pl.BlockSpec((tile, width), lambda i: (i, 0)),
            pl.BlockSpec(items.shape, lambda i: (0, 0)),
            pl.BlockSpec((1, tile), lambda i: (0, i)),
        ],
        out_specs=[
            pl.BlockSpec((tile, width), lambda i: (i, 0)),
            pl.BlockSpec((items.shape[0], width), lambda i: (0, 0)),
        ],
        out_shape=[
            jax.ShapeDtypeStruct((rows, width), jnp.float32),
            jax.ShapeDtypeStruct((items.shape[0], width), jnp.float32),
        ],
        compiler_params=pltpu.CompilerParams(
            vmem_limit_bytes=48 * 1024 * 1024, dimension_semantics=("arbitrary",)
        ),
    )(queries, items, totals)


def plane_gather(value, axis, side):
    size = side * side
    index = lax.axis_index(axis)
    column = index % side
    line = index // side

    def shift(piece, step, along_row):
        pairs = []
        for source in range(size):
            high, low = divmod(source, side)
            if along_row:
                target = high * side + (low + step) % side
            else:
                target = ((high + step) % side) * side + low
            pairs.append((source, target))
        return lax.ppermute(piece, axis, pairs)

    pieces = jnp.stack([value] + [shift(value, step, True) for step in range(1, side)])
    row = jnp.concatenate([jnp.take(pieces, (column - c) % side, axis=0) for c in range(side)], axis=1)
    rows = jnp.stack([row] + [shift(row, step, False) for step in range(1, side)])
    return jnp.concatenate([jnp.take(rows, (line - r) % side, axis=0) for r in range(side)], axis=1)


def slot_index(live_slots, positions, slot_cap):
    ending = jnp.cumsum(live_slots)
    holder = jnp.sum((ending[None, :] <= positions[:, None]).astype(jnp.int32), axis=1)
    opening = ending - live_slots
    return holder * slot_cap + positions - jnp.take(opening, holder)


def tree_sum(value, axes, inner):
    total = 1
    for axis in axes:
        total *= lax.axis_size(axis)
    index = 0
    for axis in axes:
        index = index * lax.axis_size(axis) + lax.axis_index(axis)
    step = 1
    while step < inner and step < total and value.shape[0] % 2 == 0:
        half = value.shape[0] // 2
        upper = (index & step) != 0
        keep = jnp.where(upper, value[half:], value[:half])
        send = jnp.where(upper, value[:half], value[half:])
        value = keep + lax.ppermute(send, axes, [(i, i ^ step) for i in range(total)])
        step *= 2
    halved = step
    while step < total:
        value = value + lax.ppermute(value, axes, [(i, i ^ step) for i in range(total)])
        step *= 2
    step = halved // 2
    while step >= 1:
        got = lax.ppermute(value, axes, [(i, i ^ step) for i in range(total)])
        upper = (index & step) != 0
        value = jnp.where(upper, jnp.concatenate([got, value]), jnp.concatenate([value, got]))
        step //= 2
    return value


def plane_shift(value, axis, side, step, along_row):
    pairs = []
    for source in range(side * side):
        high, low = divmod(source, side)
        if along_row:
            target = high * side + (low + step) % side
        else:
            target = ((high + step) % side) * side + low
        pairs.append((source, target))
    return lax.ppermute(value, axis, pairs)


def plane_gather_rows(value, axis, side, along_row):
    pieces = [value] + [plane_shift(value, axis, side, step, along_row) for step in range(1, side)]
    return jnp.concatenate(pieces, axis=0)


def plane_reduce_rows(value, axis, side, along_row):
    block = value.shape[0] // side
    total = value[:block]
    for step in range(1, side):
        part = value[((side - step) % side) * block:((side - step) % side + 1) * block]
        total = total + plane_shift(part, axis, side, step, along_row)
    return total


def block_grads(hidden, query_weight, item_vectors, axis, side, scaling):
    row_hidden = plane_gather_rows(hidden, axis, side, True)
    column_items = plane_gather_rows(item_vectors, axis, side, False)
    row_queries = jnp.dot(row_hidden, query_weight, preferred_element_type=jnp.float32).astype(jnp.bfloat16)
    stats = block_stats(row_queries, column_items, scaling)
    block = hidden.shape[0]
    gathered = [stats] + [
        jnp.roll(plane_shift(stats, axis, side, step, True), step * block, axis=1) for step in range(1, side)
    ]
    highest = gathered[0][0]
    for other in gathered[1:]:
        highest = jnp.maximum(highest, other[0])
    mass = gathered[0][1] * jnp.exp(gathered[0][0] - highest)
    for other in gathered[1:]:
        mass = mass + other[1] * jnp.exp(other[0] - highest)
    totals = highest + jnp.log(mass)
    pulled, pushed = block_grads_k(row_queries, column_items, totals.reshape(1, -1), scaling)
    weight_part = lax.dot_general(
        row_hidden, pulled, (((0,), (0,)), ((), ())),
        preferred_element_type=jnp.float32, precision=lax.Precision.HIGHEST,
    ) - lax.dot_general(
        hidden, item_vectors, (((0,), (0,)), ((), ())), preferred_element_type=jnp.float32
    )
    pushed = plane_reduce_rows(pushed, axis, side, False)
    item_grad = scaling * (pushed - row_queries[:block].astype(jnp.float32))
    return item_grad, scaling * weight_part


def step_body(item_table, query_table, query_weight, query_ids, fetch_rows, counts, example_pos):
    table_rows, model_width = item_table.shape
    sources = fetch_rows.shape[1]
    slot_cap = fetch_rows.shape[2]
    scaling = model_width ** (-0.5)
    requests = fetch_rows.reshape(sources, slot_cap)
    wanted = lax.all_to_all(requests, ("batch", "table"), split_axis=0, concat_axis=0, tiled=True)
    found_rows = jnp.take(item_table, wanted, axis=0)
    found_rows, query_ids = lax.optimization_barrier((found_rows, query_ids))
    fetched = lax.all_to_all(
        found_rows, ("batch", "table"), split_axis=0, concat_axis=0, tiled=True
    )
    slot_ids = slot_index(counts.reshape(sources), example_pos, slot_cap)
    item_vectors = jnp.take(fetched.reshape(sources * slot_cap, model_width), slot_ids, axis=0)
    looked = jnp.take(query_table, query_ids, axis=0).astype(jnp.float32)
    hidden = jnp.mean(looked, axis=1).astype(jnp.bfloat16)
    queries = jnp.dot(hidden, query_weight, preferred_element_type=jnp.float32).astype(jnp.bfloat16)
    side = int(round(lax.axis_size("batch") ** 0.5))
    if side * side == lax.axis_size("batch") and side > 1:
        item_grad, partial_value = block_grads(hidden, query_weight, item_vectors, "batch", side, scaling)
    else:
        group_queries = lax.all_gather(queries, "batch", axis=0, tiled=True)
        group_items = lax.all_gather(item_vectors, "batch", axis=0, tiled=True)
        query_grad, totals = forward(queries, group_items, item_vectors)
        side = int(round(lax.axis_size("batch") ** 0.5))
        if side * side == lax.axis_size("batch"):
            group_totals = plane_gather(totals[:, :1].reshape(1, -1), "batch", side)
        else:
            group_totals = lax.all_gather(totals[:, :1].reshape(1, -1), "batch", axis=1, tiled=True)
        scores_back = scaling * lax.dot_general(
            item_vectors, group_queries, (((1,), (1,)), ((), ())), preferred_element_type=jnp.float32
        )
        soft_back = jnp.exp(scores_back - group_totals).astype(jnp.bfloat16)
        summed = jnp.dot(soft_back, group_queries, preferred_element_type=jnp.float32)
        item_grad = scaling * (summed - queries.astype(jnp.float32))
        partial_value = lax.dot_general(
            hidden,
            query_grad.astype(jnp.bfloat16),
            (((0,), (0,)), ((), ())),
            preferred_element_type=jnp.float32,
        )
    total = lax.axis_size("batch") * lax.axis_size("table")
    if total & (total - 1) == 0:
        weight_grad = tree_sum(partial_value, ("batch", "table"), min(2, lax.axis_size("table")))
    else:
        weight_grad = lax.psum(partial_value, ("batch", "table"))
    item_grad, weight_grad = lax.optimization_barrier((item_grad, weight_grad))
    chosen = (lax.broadcasted_iota(jnp.int32, (sources * slot_cap, slot_ids.shape[0]), 0) == slot_ids[None, :])
    slot_grads = jnp.dot(
        chosen.astype(jnp.bfloat16), item_grad,
        preferred_element_type=jnp.float32, precision=lax.Precision.HIGHEST,
    )
    slot_grads = slot_grads.reshape(sources, slot_cap, model_width)
    returned = lax.all_to_all(
        slot_grads, ("batch", "table"), split_axis=0, concat_axis=0, tiled=True
    )
    landing = (
        lax.broadcasted_iota(jnp.int32, (table_rows, wanted.size), 0) == wanted.reshape(1, -1)
    )
    table_grad = jnp.dot(
        landing.astype(jnp.bfloat16), returned.reshape(-1, model_width),
        preferred_element_type=jnp.float32, precision=lax.Precision.HIGHEST,
    )
    return (table_grad, weight_grad)


def solution(mesh):
    in_specs = (
        P(("batch", "table"), None),
        P(),
        P(),
        P(("batch", "table"), None),
        P(("batch", "table"), None, None),
        P(("batch", "table"), None),
        P(("batch", "table")),
    )
    out_specs = (P(("batch", "table"), None), P())
    return jax.shard_map(step_body, mesh=mesh, in_specs=in_specs, out_specs=out_specs, check_vma=False)
```
